512 devices in a mesh: wide: 32 (over z, x), tensor: 16 (over y, core).
Axes of the slice: x: 4, y: 8, z: 8, core: 2. Of those that a mesh axis runs over, the one named last changes fastest.
Arguments:
- tokens: bfloat16 [16384, 8192], P('wide', 'tensor'), may hold values from -6 to 6
- key_value_weight: bfloat16 [8192, 2048], P(None, 'tensor'), may hold values from -0.0625 to 0.0625
- adapter_down_maps: bfloat16 [8192, 512, 64], P('tensor', 'wide'), may hold values from -0.0625 to 0.0625
- adapter_up_maps: bfloat16 [512, 64, 2048], P('wide', None, 'tensor'), may hold values from -0.75 to 0.75
- adapter_per_row: int32 [16384], P('wide'), may hold values from 0 to 511, as said below
- adapter_storage_slot: int32 [512], replicated, may hold values from 0 to 511, as said below
Outputs:
- kv_out: bfloat16 [16384, 2048], P('wide', 'tensor')
The draws below stay inside these ranges and needn't reach their ends.
Inputs may be any that keep to these rules, and one draw needn't show every extreme that they name: `adapter_per_row`: the adapter stored at position p belongs to owner p // 16 of wide. Among the 512 rows of one index of wide, at most 32 name adapters of one owner; in every draw one owner gets exactly 32 rows from every index of wide. `adapter_storage_slot`: each position is taken by exactly one adapter.
All inputs are finite; a program needn't handle non-finite values.
Results may differ from the reference program's by a relative error of at most 0.0049.
Values may be sent and summed in bfloat16 or wider, within the bound.
No kernel may reach another device: no remote copies, remote signals or barrier semaphores. Data moves between devices by JAX's collectives and lax.ppermute only.
A program may use at most 64 MiB of HBM per device.

```python
import jax
import jax.numpy as jnp
from jax import lax

MODEL_WIDTH = 8192
KEY_VALUE_COLUMNS = 2048
ADAPTER_RANK = 64
TOK_DEV = 512
ADP_DEV = 16
TOKENS = 16384
ADAPTER_COUNT = 512
CAP = 32


def common_draw(key):
    base_key = jax.random.fold_in(key, 7)
    wide_count = TOKENS // TOK_DEV
    place = jax.random.permutation(jax.random.fold_in(base_key, 1), ADAPTER_COUNT).astype(jnp.int32)
    hottest = jax.random.randint(jax.random.fold_in(base_key, 2), (), 0, wide_count)

    def block_positions(block):
        block_key = jax.random.fold_in(base_key, 100 + block)
        others = jax.random.permutation(jax.random.fold_in(block_key, 1), (wide_count - 1) * CAP)[:TOK_DEV - CAP] + CAP
        virtual = jnp.concatenate([jnp.arange(CAP, dtype=jnp.int32), others.astype(jnp.int32)])
        virtual = jax.random.permutation(jax.random.fold_in(block_key, 2), virtual)
        owner_index = (virtual // CAP + hottest) % wide_count
        local_index = jax.random.randint(jax.random.fold_in(block_key, 3), (TOK_DEV,), 0, ADP_DEV)
        return (owner_index * ADP_DEV + local_index).astype(jnp.int32)
    positions = jax.vmap(block_positions)(jnp.arange(wide_count)).reshape(TOKENS)
    inverse = jnp.zeros((ADAPTER_COUNT,), jnp.int32).at[place].set(jnp.arange(ADAPTER_COUNT, dtype=jnp.int32))
    return (place, inverse[positions].astype(jnp.int32))


def draw_adapter_per_row(key, part):
    return common_draw(key)[1]


def draw_adapter_storage_slot(key, part):
    return common_draw(key)[0]


def shard_levels(stream_key, shape, cuts, least, high):
    def one(axis_at, parts):
        steps = jax.random.uniform(jax.random.fold_in(jax.random.fold_in(stream_key, 6), axis_at), (parts,), jnp.float32, least / len(cuts), high / len(cuts))
        return jnp.repeat(jnp.exp(steps), shape[axis_at] // parts).reshape((-1,) + (1,) * (len(shape) - axis_at - 1))

    gain = one(*cuts[0])
    for cut in cuts[1:]:
        gain = gain * one(*cut)
    return gain


def centred(rng, shape, width, bound, split=(), kind=jnp.bfloat16):
    values = width * jax.random.normal(rng, shape, jnp.float32)
    if split:
        values = values * shard_levels(rng, shape, split, -0.22, 0.18)
    return jnp.clip(values, -bound, bound).astype(kind)


def setup_inputs(seed: int = 0) -> dict:
    key_of = jax.random.split(jax.random.key(seed), 7)
    return {
        "tokens": centred(key_of[0], (TOKENS, MODEL_WIDTH), 1.0, 6.0, ((0, 32), (1, 16))),
        "key_value_weight": centred(key_of[1], (MODEL_WIDTH, KEY_VALUE_COLUMNS), MODEL_WIDTH ** -0.5, 0.0625, ((1, 16),)),
        "adapter_down_maps": centred(key_of[2], (MODEL_WIDTH, ADAPTER_COUNT, ADAPTER_RANK), MODEL_WIDTH ** -0.5, 0.0625, ((0, 16), (1, 32))),
        "adapter_up_maps": centred(key_of[3], (ADAPTER_COUNT, ADAPTER_RANK, KEY_VALUE_COLUMNS), ADAPTER_RANK ** -0.5, 0.75, ((0, 32), (2, 16))),
        "adapter_per_row": draw_adapter_per_row(jax.random.fold_in(key_of[6], 71), 0),
        "adapter_storage_slot": draw_adapter_storage_slot(jax.random.fold_in(key_of[6], 71), 0),
    }


def reference(tokens, key_value_weight, adapter_down_maps, adapter_up_maps, adapter_per_row, adapter_storage_slot):
    base_projection_output = jnp.dot(tokens, key_value_weight, preferred_element_type=jnp.float32)
    storage_position = adapter_storage_slot[adapter_per_row].astype(jnp.int32)

    def single_row(pair):
        token_row, storage_index = pair
        down_matrix = lax.dynamic_index_in_dim(adapter_down_maps, storage_index, 1, keepdims=False)
        reduced_rows = jnp.dot(token_row[None, :], down_matrix, preferred_element_type=jnp.float32).astype(jnp.bfloat16)
        up_matrix = lax.dynamic_index_in_dim(adapter_up_maps, storage_index, 0, keepdims=False)
        adapter_correction = jnp.dot(reduced_rows, up_matrix, preferred_element_type=jnp.float32).astype(jnp.bfloat16)
        return adapter_correction[0]

    adapter_correction = lax.map(single_row, (tokens, storage_position))
    return (base_projection_output + adapter_correction.astype(jnp.float32)).astype(jnp.bfloat16)
```

```python
import jax
import jax.numpy as jnp
from jax import lax
from jax.sharding import PartitionSpec as P


def body(
    tokens,
    key_value_weight,
    adapter_down_maps,
    adapter_up_maps,
    adapter_per_row,
    adapter_storage_slot,
):
    row_count, feature_portion = tokens.shape
    wide_count = lax.axis_size("wide")
    capacity = 2 * row_count // wide_count
    present_adapters = adapter_down_maps.shape[1]
    rank_dimension = adapter_down_maps.shape[2]
    column_portion = key_value_weight.shape[1]
    total_adapters = adapter_storage_slot.shape[0]
    slot_count = wide_count * capacity
    lane = 128

    gathered = lax.all_gather(tokens, "tensor", axis=1, tiled=True)
    base_projection_output = jnp.dot(
        gathered, key_value_weight, preferred_element_type=jnp.float32
    )

    storage_position = jnp.take(adapter_storage_slot, adapter_per_row, axis=0)
    owner_index = storage_position // present_adapters
    local_index = storage_position % present_adapters

    owner_onehot = (
        owner_index[:, None] == jnp.arange(wide_count, dtype=jnp.int32)[None, :]
    ).astype(jnp.float32)
    row_iota = jnp.arange(row_count, dtype=jnp.int32)
    strictly_before = (row_iota[:, None] > row_iota[None, :]).astype(jnp.float32)
    earlier = jnp.dot(strictly_before, owner_onehot, preferred_element_type=jnp.float32)
    rank_in_owner = jnp.sum(earlier * owner_onehot, axis=1).astype(jnp.int32)
    destination = owner_index * capacity + rank_in_owner

    placement = (
        jnp.arange(slot_count, dtype=jnp.int32)[:, None] == destination[None, :]
    ).astype(jnp.bfloat16)

    local_onehot = (
        local_index[:, None] == jnp.arange(lane, dtype=jnp.int32)[None, :]
    ).astype(jnp.bfloat16)
    extended = jnp.concatenate([tokens, local_onehot], axis=1)
    send_rows = jnp.dot(placement, extended, preferred_element_type=jnp.float32).astype(
        jnp.bfloat16
    )
    send_rows = send_rows.reshape(wide_count, capacity, feature_portion + lane)

    got_rows = lax.all_to_all(send_rows, "wide", split_axis=0, concat_axis=0, tiled=True)
    got_rows = got_rows.reshape(slot_count, feature_portion + lane)
    flat_rows = got_rows[:, :feature_portion]
    got_onehot = got_rows[:, feature_portion : feature_portion + present_adapters]

    down_matrix = adapter_down_maps.reshape(feature_portion, present_adapters * rank_dimension)
    all_ranks = jnp.dot(flat_rows, down_matrix, preferred_element_type=jnp.float32)
    all_ranks = all_ranks.reshape(slot_count, present_adapters, rank_dimension)
    selected = got_onehot[:, :, None] > 0
    partial_value = jnp.sum(jnp.where(selected, all_ranks, 0.0), axis=1)
    summed = partial_value
    tensor_count = lax.axis_size("tensor")
    step = 1
    while step < tensor_count:
        exchange = [(i, i ^ step) for i in range(tensor_count)]
        summed = summed + lax.ppermute(summed, "tensor", exchange)
        step *= 2
    reduced_rows = summed.astype(jnp.bfloat16)

    expanded_rows = jnp.where(
        selected, reduced_rows[:, None, :], jnp.zeros((), jnp.bfloat16)
    ).reshape(slot_count, present_adapters * rank_dimension)
    up_matrix = adapter_up_maps.reshape(present_adapters * rank_dimension, column_portion)
    adapter_correction = jnp.dot(
        expanded_rows, up_matrix, preferred_element_type=jnp.float32
    ).astype(jnp.bfloat16)
    adapter_correction = adapter_correction.reshape(wide_count, capacity, column_portion)
    returned_rows = lax.all_to_all(
        adapter_correction, "wide", split_axis=0, concat_axis=0, tiled=True
    )
    returned_rows = returned_rows.reshape(slot_count, column_portion)
    adapter_row_output = jnp.dot(
        placement.T, returned_rows, preferred_element_type=jnp.float32
    )
    return (base_projection_output + adapter_row_output).astype(jnp.bfloat16)


def solution(mesh):
    in_specs = (
        P("wide", "tensor"),
        P(None, "tensor"),
        P("tensor", "wide", None),
        P("wide", None, "tensor"),
        P("wide"),
        P(),
    )
    out_specs = P("wide", "tensor")
    return jax.shard_map(body, mesh=mesh, in_specs=in_specs, out_specs=out_specs, check_vma=False)
```

```python
import jax
import jax.numpy as jnp
from jax import lax
from jax.sharding import PartitionSpec as P


def tensor_sum(partial_value, tensor_count):
    position = lax.axis_index("tensor")
    block = partial_value
    steps = []
    step = 1
    while step < tensor_count:
        half = block.shape[0] // 2
        upper = (position // step) % 2
        low_part = block[:half]
        high_part = block[half:]
        keep = jnp.where(upper == 1, high_part, low_part)
        send = jnp.where(upper == 1, low_part, high_part)
        exchange = [(i, i ^ step) for i in range(tensor_count)]
        block = keep + lax.ppermute(send, "tensor", exchange)
        steps.append((step, upper))
        step *= 2
    block = block.astype(jnp.bfloat16)
    for step, upper in reversed(steps):
        exchange = [(i, i ^ step) for i in range(tensor_count)]
        other = lax.ppermute(block, "tensor", exchange)
        block = jnp.where(
            upper == 1,
            jnp.concatenate([other, block], axis=0),
            jnp.concatenate([block, other], axis=0),
        )
    return block


def body(
    tokens,
    key_value_weight,
    adapter_down_maps,
    adapter_up_maps,
    adapter_per_row,
    adapter_storage_slot,
):
    row_count, feature_portion = tokens.shape
    wide_count = lax.axis_size("wide")
    tensor_count = lax.axis_size("tensor")
    capacity = 2 * row_count // wide_count
    present_adapters = adapter_down_maps.shape[1]
    rank_dimension = adapter_down_maps.shape[2]
    column_portion = key_value_weight.shape[1]
    total_adapters = adapter_storage_slot.shape[0]
    slot_count = wide_count * capacity
    lane = 128
    row_tiles = capacity * feature_portion // lane
    info_rows = 8

    gathered = lax.all_gather(tokens, "tensor", axis=1, tiled=True)
    base_projection_output = jnp.dot(
        gathered, key_value_weight, preferred_element_type=jnp.float32
    )

    adapter_match = adapter_per_row[:, None] == jnp.arange(total_adapters, dtype=jnp.int32)[None, :]
    storage_position = jnp.sum(jnp.where(adapter_match, adapter_storage_slot[None, :], 0), axis=1)
    owner_index = storage_position // present_adapters
    local_index = storage_position % present_adapters

    owner_onehot = (
        owner_index[:, None] == jnp.arange(wide_count, dtype=jnp.int32)[None, :]
    ).astype(jnp.float32)
    row_iota = jnp.arange(row_count, dtype=jnp.int32)
    strictly_before = (row_iota[:, None] > row_iota[None, :]).astype(jnp.float32)
    earlier = jnp.dot(strictly_before, owner_onehot, preferred_element_type=jnp.float32)
    rank_in_owner = jnp.sum(earlier * owner_onehot, axis=1).astype(jnp.int32)
    destination = owner_index * capacity + rank_in_owner

    placement = (
        jnp.arange(slot_count, dtype=jnp.int32)[:, None] == destination[None, :]
    ).astype(jnp.bfloat16)

    local_code = jnp.broadcast_to(
        (local_index + 1).astype(jnp.bfloat16)[:, None], (row_count, lane)
    )
    extended = jnp.concatenate([tokens, local_code], axis=1)
    placed = jnp.dot(placement, extended, preferred_element_type=jnp.float32).astype(
        jnp.bfloat16
    )
    send_rows = placed[:, :feature_portion].reshape(wide_count, row_tiles, lane)
    slot_code = placed[:, feature_portion].reshape(wide_count, 1, capacity)
    slot_code = jnp.pad(slot_code, ((0, 0), (0, info_rows - 1), (0, lane - capacity)))
    send_block = jnp.concatenate([send_rows, slot_code], axis=1)

    got_block = lax.all_to_all(send_block, "wide", split_axis=0, concat_axis=0, tiled=True)
    flat_rows = got_block[:, :row_tiles, :].reshape(slot_count, feature_portion)
    got_code = got_block[:, row_tiles, :capacity].reshape(slot_count).astype(jnp.int32)
    selected = (
        got_code[:, None] == jnp.arange(1, present_adapters + 1, dtype=jnp.int32)[None, :]
    )[:, :, None]

    down_matrix = adapter_down_maps.reshape(feature_portion, present_adapters * rank_dimension)
    all_ranks = jnp.dot(flat_rows, down_matrix, preferred_element_type=jnp.float32)
    all_ranks = all_ranks.reshape(slot_count, present_adapters, rank_dimension)
    partial_value = jnp.sum(jnp.where(selected, all_ranks, 0.0), axis=1)
    reduced_rows = tensor_sum(partial_value, tensor_count)

    expanded_rows = jnp.where(
        selected, reduced_rows[:, None, :], jnp.zeros((), jnp.bfloat16)
    ).reshape(slot_count, present_adapters * rank_dimension)
    up_matrix = adapter_up_maps.reshape(present_adapters * rank_dimension, column_portion)
    adapter_correction = jnp.dot(
        expanded_rows, up_matrix, preferred_element_type=jnp.float32
    ).astype(jnp.bfloat16)
    adapter_correction = adapter_correction.reshape(wide_count, capacity, column_portion)
    returned_rows = lax.all_to_all(
        adapter_correction, "wide", split_axis=0, concat_axis=0, tiled=True
    )
    returned_rows = returned_rows.reshape(slot_count, column_portion)
    adapter_row_output = jnp.dot(
        placement.T, returned_rows, preferred_element_type=jnp.float32
    )
    return (base_projection_output + adapter_row_output).astype(jnp.bfloat16)


def solution(mesh):
    in_specs = (
        P("wide", "tensor"),
        P(None, "tensor"),
        P("tensor", "wide", None),
        P("wide", None, "tensor"),
        P("wide"),
        P(),
    )
    out_specs = P("wide", "tensor")
    return jax.shard_map(body, mesh=mesh, in_specs=in_specs, out_specs=out_specs, check_vma=False)
```

```python
import jax
import jax.numpy as jnp
from jax import lax
from jax.sharding import PartitionSpec as P


def tensor_sum(partial_value, tensor_count):
    position = lax.axis_index("tensor")
    block = partial_value
    steps = []
    step = 1
    while step < tensor_count:
        half = block.shape[0] // 2
        upper = (position // step) % 2
        low_part = block[:half]
        high_part = block[half:]
        keep = jnp.where(upper == 1, high_part, low_part)
        send = jnp.where(upper == 1, low_part, high_part)
        exchange = [(i, i ^ step) for i in range(tensor_count)]
        block = keep + lax.ppermute(send, "tensor", exchange)
        steps.append((step, upper))
        step *= 2
    block = block.astype(jnp.bfloat16)
    for step, upper in reversed(steps):
        exchange = [(i, i ^ step) for i in range(tensor_count)]
        other = lax.ppermute(block, "tensor", exchange)
        block = jnp.where(
            upper == 1,
            jnp.concatenate([other, block], axis=0),
            jnp.concatenate([block, other], axis=0),
        )
    return block


def body(
    tokens,
    key_value_weight,
    adapter_down_maps,
    adapter_up_maps,
    adapter_per_row,
    adapter_storage_slot,
):
    row_count, feature_portion = tokens.shape
    wide_count = lax.axis_size("wide")
    tensor_count = lax.axis_size("tensor")
    capacity = 2 * row_count // wide_count
    present_adapters = adapter_down_maps.shape[1]
    rank_dimension = adapter_down_maps.shape[2]
    column_portion = key_value_weight.shape[1]
    total_adapters = adapter_storage_slot.shape[0]
    slot_count = wide_count * capacity
    lane = 128
    row_tiles = capacity * feature_portion // lane
    info_rows = 8

    gathered = lax.all_gather(tokens, "tensor", axis=1, tiled=True)
    base_projection_output = jnp.dot(
        gathered, key_value_weight, preferred_element_type=jnp.float32
    )

    adapter_match = adapter_per_row[:, None] == jnp.arange(total_adapters, dtype=jnp.int32)[None, :]
    storage_position = jnp.sum(jnp.where(adapter_match, adapter_storage_slot[None, :], 0), axis=1)
    owner_index = storage_position // present_adapters
    local_index = storage_position % present_adapters

    owner_onehot = (
        owner_index[:, None] == jnp.arange(wide_count, dtype=jnp.int32)[None, :]
    ).astype(jnp.float32)
    row_iota = jnp.arange(row_count, dtype=jnp.int32)
    strictly_before = (row_iota[:, None] > row_iota[None, :]).astype(jnp.float32)
    earlier = jnp.dot(strictly_before, owner_onehot, preferred_element_type=jnp.float32)
    rank_in_owner = jnp.sum(earlier * owner_onehot, axis=1).astype(jnp.int32)
    destination = owner_index * capacity + rank_in_owner

    placement = (
        jnp.arange(slot_count, dtype=jnp.int32)[:, None] == destination[None, :]
    ).astype(jnp.bfloat16)

    local_code = jnp.broadcast_to(
        (local_index + 1).astype(jnp.bfloat16)[:, None], (row_count, lane)
    )
    extended = jnp.concatenate([tokens, local_code], axis=1)
    placed = jnp.dot(placement, extended, preferred_element_type=jnp.float32).astype(
        jnp.bfloat16
    )
    send_rows = placed[:, :feature_portion].reshape(wide_count, row_tiles, lane)
    slot_code = placed[:, feature_portion].reshape(wide_count, 1, capacity)
    slot_code = jnp.pad(slot_code, ((0, 0), (0, info_rows - 1), (0, lane - capacity)))
    send_block = jnp.concatenate([send_rows, slot_code], axis=1)

    got_block = lax.all_to_all(send_block, "wide", split_axis=0, concat_axis=0, tiled=True)
    flat_rows = got_block[:, :row_tiles, :].reshape(slot_count, feature_portion)
    got_code = got_block[:, row_tiles, :capacity].reshape(slot_count).astype(jnp.int32)
    selected = (
        got_code[:, None] == jnp.arange(1, present_adapters + 1, dtype=jnp.int32)[None, :]
    )[:, :, None]

    down_matrix = adapter_down_maps.reshape(feature_portion, present_adapters * rank_dimension)
    all_ranks = jnp.dot(flat_rows, down_matrix, preferred_element_type=jnp.float32)
    all_ranks = all_ranks.reshape(slot_count, present_adapters, rank_dimension)
    partial_value = jnp.sum(jnp.where(selected, all_ranks, 0.0), axis=1)
    ordered = partial_value + 0.0 * gathered[0, 0].astype(jnp.float32)
    scattered = lax.psum_scatter(ordered, "tensor", scatter_dimension=0, tiled=True)
    wide_block = jnp.pad(scattered.astype(jnp.bfloat16), ((0, 0), (0, 448)))
    reduced_rows = lax.all_gather(wide_block, "tensor", axis=0, tiled=True)[:, :64]

    expanded_rows = jnp.where(
        selected, reduced_rows[:, None, :], jnp.zeros((), jnp.bfloat16)
    ).reshape(slot_count, present_adapters * rank_dimension)
    up_matrix = adapter_up_maps.reshape(present_adapters * rank_dimension, column_portion)
    adapter_correction = jnp.dot(
        expanded_rows, up_matrix, preferred_element_type=jnp.float32
    ).astype(jnp.bfloat16)
    adapter_correction = adapter_correction.reshape(wide_count, capacity, column_portion)
    returned_rows = lax.all_to_all(
        adapter_correction, "wide", split_axis=0, concat_axis=0, tiled=True
    )
    returned_rows = returned_rows.reshape(slot_count, column_portion)
    adapter_row_output = jnp.dot(
        placement.T, returned_rows, preferred_element_type=jnp.float32
    )
    return (base_projection_output + adapter_row_output).astype(jnp.bfloat16)


def solution(mesh):
    in_specs = (
        P("wide", "tensor"),
        P(None, "tensor"),
        P("tensor", "wide", None),
        P("wide", None, "tensor"),
        P("wide"),
        P(),
    )
    out_specs = P("wide", "tensor")
    return jax.shard_map(body, mesh=mesh, in_specs=in_specs, out_specs=out_specs, check_vma=False)
```

```python
import jax
import jax.numpy as jnp
from jax import lax
from jax.sharding import PartitionSpec as P


def body(
    tokens,
    key_value_weight,
    adapter_down_maps,
    adapter_up_maps,
    adapter_per_row,
    adapter_storage_slot,
):
    row_count, feature_portion = tokens.shape
    wide_count = lax.axis_size("wide")
    tensor_count = lax.axis_size("tensor")
    capacity = 2 * row_count // wide_count
    present_adapters = adapter_down_maps.shape[1]
    rank_dimension = adapter_down_maps.shape[2]
    column_portion = key_value_weight.shape[1]
    total_adapters = adapter_storage_slot.shape[0]
    slot_count = wide_count * capacity
    lane = 128
    row_tiles = capacity * feature_portion // lane
    info_rows = 8

    gathered = lax.all_gather(tokens, "tensor", axis=1, tiled=True)
    base_projection_output = jnp.dot(
        gathered, key_value_weight, preferred_element_type=jnp.float32
    )

    adapter_match = adapter_per_row[:, None] == jnp.arange(total_adapters, dtype=jnp.int32)[None, :]
    storage_position = jnp.sum(jnp.where(adapter_match, adapter_storage_slot[None, :], 0), axis=1)
    owner_index = storage_position // present_adapters
    local_index = storage_position % present_adapters

    owner_onehot = (
        owner_index[:, None] == jnp.arange(wide_count, dtype=jnp.int32)[None, :]
    ).astype(jnp.float32)
    row_iota = jnp.arange(row_count, dtype=jnp.int32)
    strictly_before = (row_iota[:, None] > row_iota[None, :]).astype(jnp.float32)
    earlier = jnp.dot(strictly_before, owner_onehot, preferred_element_type=jnp.float32)
    rank_in_owner = jnp.sum(earlier * owner_onehot, axis=1).astype(jnp.int32)
    destination = owner_index * capacity + rank_in_owner

    placement = (
        jnp.arange(slot_count, dtype=jnp.int32)[:, None] == destination[None, :]
    ).astype(jnp.bfloat16)

    local_code = jnp.broadcast_to(
        (local_index + 1).astype(jnp.bfloat16)[:, None], (row_count, lane)
    )
    extended = jnp.concatenate([tokens, local_code], axis=1)
    placed = jnp.dot(placement, extended, preferred_element_type=jnp.float32).astype(
        jnp.bfloat16
    )
    send_rows = placed[:, :feature_portion].reshape(wide_count, row_tiles, lane)
    slot_code = placed[:, feature_portion].reshape(wide_count, 1, capacity)
    slot_code = jnp.pad(slot_code, ((0, 0), (0, info_rows - 1), (0, lane - capacity)))
    send_block = jnp.concatenate([send_rows, slot_code], axis=1)

    got_block = lax.all_to_all(send_block, "wide", split_axis=0, concat_axis=0, tiled=True)
    flat_rows = got_block[:, :row_tiles, :].reshape(slot_count, feature_portion)
    got_code = got_block[:, row_tiles, :capacity].reshape(slot_count).astype(jnp.int32)
    selected = (
        got_code[:, None] == jnp.arange(1, present_adapters + 1, dtype=jnp.int32)[None, :]
    )[:, :, None]

    down_matrix = adapter_down_maps.reshape(feature_portion, present_adapters * rank_dimension)
    all_ranks = jnp.dot(flat_rows, down_matrix, preferred_element_type=jnp.float32)
    all_ranks = all_ranks.reshape(slot_count, present_adapters, rank_dimension)
    partial_value = jnp.sum(jnp.where(selected, all_ranks, 0.0), axis=1)
    slot_blocks = partial_value.reshape(tensor_count, slot_count // tensor_count, rank_dimension)
    gathered_blocks = lax.all_to_all(slot_blocks, "tensor", split_axis=0, concat_axis=0, tiled=True)
    own_sum = jnp.sum(gathered_blocks, axis=0).astype(jnp.bfloat16)
    spread = jnp.broadcast_to(own_sum[None], (tensor_count,) + own_sum.shape)
    reduced_rows = lax.all_to_all(spread, "tensor", split_axis=0, concat_axis=0, tiled=True)
    reduced_rows = reduced_rows.reshape(slot_count, rank_dimension)

    expanded_rows = jnp.where(
        selected, reduced_rows[:, None, :], jnp.zeros((), jnp.bfloat16)
    ).reshape(slot_count, present_adapters * rank_dimension)
    up_matrix = adapter_up_maps.reshape(present_adapters * rank_dimension, column_portion)
    adapter_correction = jnp.dot(
        expanded_rows, up_matrix, preferred_element_type=jnp.float32
    ).astype(jnp.bfloat16)
    adapter_correction = adapter_correction.reshape(wide_count, capacity, column_portion)
    returned_rows = lax.all_to_all(
        adapter_correction, "wide", split_axis=0, concat_axis=0, tiled=True
    )
    returned_rows = returned_rows.reshape(slot_count, column_portion)
    adapter_row_output = jnp.dot(
        placement.T, returned_rows, preferred_element_type=jnp.float32
    )
    return (base_projection_output + adapter_row_output).astype(jnp.bfloat16)


def solution(mesh):
    in_specs = (
        P("wide", "tensor"),
        P(None, "tensor"),
        P("tensor", "wide", None),
        P("wide", None, "tensor"),
        P("wide"),
        P(),
    )
    out_specs = P("wide", "tensor")
    return jax.shard_map(body, mesh=mesh, in_specs=in_specs, out_specs=out_specs, check_vma=False)
```

```python
import jax
import jax.numpy as jnp
from jax import lax
from jax.sharding import PartitionSpec as P


def body(
    tokens,
    key_value_weight,
    adapter_down_maps,
    adapter_up_maps,
    adapter_per_row,
    adapter_storage_slot,
):
    row_count, feature_portion = tokens.shape
    wide_count = lax.axis_size("wide")
    tensor_count = lax.axis_size("tensor")
    capacity = 2 * row_count // wide_count
    present_adapters = adapter_down_maps.shape[1]
    rank_dimension = adapter_down_maps.shape[2]
    column_portion = key_value_weight.shape[1]
    total_adapters = adapter_storage_slot.shape[0]
    slot_count = wide_count * capacity
    lane = 128
    info_rows = 8

    gathered = lax.all_gather(tokens, "tensor", axis=1, tiled=True)
    base_projection_output = jnp.dot(
        gathered, key_value_weight, preferred_element_type=jnp.float32
    )

    adapter_match = adapter_per_row[:, None] == jnp.arange(total_adapters, dtype=jnp.int32)[None, :]
    storage_position = jnp.sum(jnp.where(adapter_match, adapter_storage_slot[None, :], 0), axis=1)
    owner_index = storage_position // present_adapters
    local_index = storage_position % present_adapters

    owner_onehot = (
        owner_index[:, None] == jnp.arange(wide_count, dtype=jnp.int32)[None, :]
    ).astype(jnp.float32)
    row_iota = jnp.arange(row_count, dtype=jnp.int32)
    strictly_before = (row_iota[:, None] > row_iota[None, :]).astype(jnp.float32)
    earlier = jnp.dot(strictly_before, owner_onehot, preferred_element_type=jnp.float32)
    rank_in_owner = jnp.sum(earlier * owner_onehot, axis=1).astype(jnp.int32)
    destination = owner_index * capacity + rank_in_owner

    placement = (
        jnp.arange(slot_count, dtype=jnp.int32)[:, None] == destination[None, :]
    ).astype(jnp.bfloat16)

    lane_tiles = feature_portion // lane
    local_code = jnp.broadcast_to(
        (local_index + 1).astype(jnp.bfloat16)[:, None], (row_count, lane)
    )
    pieces = []
    for tile in range(lane_tiles):
        placed = jnp.dot(
            placement, tokens[:, tile * lane : (tile + 1) * lane],
            preferred_element_type=jnp.float32,
        ).astype(jnp.bfloat16)
        pieces.append(placed.reshape(wide_count, capacity, lane))
    placed_code = jnp.dot(placement, local_code, preferred_element_type=jnp.float32)
    slot_code = placed_code[:, 0].astype(jnp.bfloat16).reshape(wide_count, 1, capacity)
    pieces.append(jnp.pad(slot_code, ((0, 0), (0, info_rows - 1), (0, lane - capacity))))
    send_block = jnp.concatenate(pieces, axis=1)

    got_block = lax.all_to_all(send_block, "wide", split_axis=0, concat_axis=0, tiled=True)
    flat_rows = jnp.concatenate(
        [
            got_block[:, tile * capacity : (tile + 1) * capacity, :].reshape(slot_count, lane)
            for tile in range(lane_tiles)
        ],
        axis=1,
    )
    got_code = (
        got_block[:, lane_tiles * capacity, :capacity].reshape(slot_count).astype(jnp.int32)
    )
    selected = (
        got_code[:, None] == jnp.arange(1, present_adapters + 1, dtype=jnp.int32)[None, :]
    )[:, :, None]

    down_matrix = adapter_down_maps.reshape(feature_portion, present_adapters * rank_dimension)
    all_ranks = jnp.dot(flat_rows, down_matrix, preferred_element_type=jnp.float32)
    all_ranks = all_ranks.reshape(slot_count, present_adapters, rank_dimension)
    partial_value = jnp.sum(jnp.where(selected, all_ranks, 0.0), axis=1)
    slot_blocks = partial_value.reshape(tensor_count, slot_count // tensor_count, rank_dimension)
    gathered_blocks = lax.all_to_all(slot_blocks, "tensor", split_axis=0, concat_axis=0, tiled=True)
    own_sum = jnp.sum(gathered_blocks, axis=0).astype(jnp.bfloat16)
    spread = jnp.broadcast_to(own_sum[None], (tensor_count,) + own_sum.shape)
    reduced_rows = lax.all_to_all(spread, "tensor", split_axis=0, concat_axis=0, tiled=True)
    reduced_rows = reduced_rows.reshape(slot_count, rank_dimension)

    expanded_rows = jnp.where(
        selected, reduced_rows[:, None, :], jnp.zeros((), jnp.bfloat16)
    ).reshape(slot_count, present_adapters * rank_dimension)
    up_matrix = adapter_up_maps.reshape(present_adapters * rank_dimension, column_portion)
    adapter_correction = jnp.dot(
        expanded_rows, up_matrix, preferred_element_type=jnp.float32
    ).astype(jnp.bfloat16)
    adapter_correction = adapter_correction.reshape(wide_count, capacity, column_portion)
    returned_rows = lax.all_to_all(
        adapter_correction, "wide", split_axis=0, concat_axis=0, tiled=True
    )
    returned_rows = returned_rows.reshape(slot_count, column_portion)
    adapter_row_output = jnp.dot(
        placement.T, returned_rows, preferred_element_type=jnp.float32
    )
    return (base_projection_output + adapter_row_output).astype(jnp.bfloat16)


def solution(mesh):
    in_specs = (
        P("wide", "tensor"),
        P(None, "tensor"),
        P("tensor", "wide", None),
        P("wide", None, "tensor"),
        P("wide"),
        P(),
    )
    out_specs = P("wide", "tensor")
    return jax.shard_map(body, mesh=mesh, in_specs=in_specs, out_specs=out_specs, check_vma=False)
```

```python
import jax
import jax.numpy as jnp
from jax import lax
from jax.sharding import PartitionSpec as P


def body(
    tokens,
    key_value_weight,
    adapter_down_maps,
    adapter_up_maps,
    adapter_per_row,
    adapter_storage_slot,
):
    row_count, feature_portion = tokens.shape
    wide_count = lax.axis_size("wide")
    tensor_count = lax.axis_size("tensor")
    capacity = 2 * row_count // wide_count
    present_adapters = adapter_down_maps.shape[1]
    rank_dimension = adapter_down_maps.shape[2]
    column_portion = key_value_weight.shape[1]
    total_adapters = adapter_storage_slot.shape[0]
    slot_count = wide_count * capacity
    lane = 128
    info_rows = 8

    gathered = lax.all_gather(tokens, "tensor", axis=1, tiled=True)
    base_projection_output = jnp.dot(
        gathered, key_value_weight, preferred_element_type=jnp.float32
    )

    adapter_match = adapter_per_row[:, None] == jnp.arange(total_adapters, dtype=jnp.int32)[None, :]
    storage_position = jnp.sum(jnp.where(adapter_match, adapter_storage_slot[None, :], 0), axis=1)
    owner_index = storage_position // present_adapters
    local_index = storage_position % present_adapters

    owner_onehot = (
        owner_index[:, None] == jnp.arange(wide_count, dtype=jnp.int32)[None, :]
    ).astype(jnp.float32)
    row_iota = jnp.arange(row_count, dtype=jnp.int32)
    strictly_before = (row_iota[:, None] > row_iota[None, :]).astype(jnp.float32)
    earlier = jnp.dot(strictly_before, owner_onehot, preferred_element_type=jnp.float32)
    rank_in_owner = jnp.sum(earlier * owner_onehot, axis=1).astype(jnp.int32)
    destination = owner_index * capacity + rank_in_owner

    placement = (
        jnp.arange(slot_count, dtype=jnp.int32)[:, None] == destination[None, :]
    ).astype(jnp.bfloat16)

    lane_tiles = feature_portion // lane
    local_code = jnp.broadcast_to(
        (local_index + 1).astype(jnp.bfloat16)[:, None], (row_count, lane)
    )
    pieces = []
    for tile in range(lane_tiles):
        placed = jnp.dot(
            placement, tokens[:, tile * lane : (tile + 1) * lane],
            preferred_element_type=jnp.float32,
        ).astype(jnp.bfloat16)
        pieces.append(placed.reshape(wide_count, capacity, lane))
    placed_code = jnp.dot(placement, local_code, preferred_element_type=jnp.float32)
    slot_code = placed_code[:, 0].astype(jnp.bfloat16).reshape(wide_count, 1, capacity)
    pieces.append(jnp.pad(slot_code, ((0, 0), (0, info_rows - 1), (0, lane - capacity))))
    send_block = jnp.concatenate(pieces, axis=1)

    got_block = lax.all_to_all(send_block, "wide", split_axis=0, concat_axis=0, tiled=True)
    flat_rows = jnp.concatenate(
        [
            got_block[:, tile * capacity : (tile + 1) * capacity, :].reshape(slot_count, lane)
            for tile in range(lane_tiles)
        ],
        axis=1,
    )
    got_code = (
        got_block[:, lane_tiles * capacity, :capacity].reshape(slot_count).astype(jnp.int32)
    )
    selected = (
        got_code[:, None] == jnp.arange(1, present_adapters + 1, dtype=jnp.int32)[None, :]
    )[:, :, None]

    down_matrix = adapter_down_maps.reshape(feature_portion, present_adapters * rank_dimension)
    all_ranks = jnp.dot(flat_rows, down_matrix, preferred_element_type=jnp.float32)
    all_ranks = all_ranks.reshape(slot_count, present_adapters, rank_dimension)
    partial_value = jnp.sum(jnp.where(selected, all_ranks, 0.0), axis=1)
    slot_blocks = partial_value.reshape(tensor_count, slot_count // tensor_count, rank_dimension)
    gathered_blocks = lax.all_to_all(
        slot_blocks.astype(jnp.bfloat16), "tensor", split_axis=0, concat_axis=0, tiled=True
    )
    own_sum = jnp.sum(gathered_blocks.astype(jnp.float32), axis=0).astype(jnp.bfloat16)
    spread = jnp.broadcast_to(own_sum[None], (tensor_count,) + own_sum.shape)
    reduced_rows = lax.all_to_all(spread, "tensor", split_axis=0, concat_axis=0, tiled=True)
    reduced_rows = reduced_rows.reshape(slot_count, rank_dimension)

    expanded_rows = jnp.where(
        selected, reduced_rows[:, None, :], jnp.zeros((), jnp.bfloat16)
    ).reshape(slot_count, present_adapters * rank_dimension)
    up_matrix = adapter_up_maps.reshape(present_adapters * rank_dimension, column_portion)
    adapter_correction = jnp.dot(
        expanded_rows, up_matrix, preferred_element_type=jnp.float32
    ).astype(jnp.bfloat16)
    adapter_correction = adapter_correction.reshape(wide_count, capacity, column_portion)
    returned_rows = lax.all_to_all(
        adapter_correction, "wide", split_axis=0, concat_axis=0, tiled=True
    )
    returned_rows = returned_rows.reshape(slot_count, column_portion)
    adapter_row_output = jnp.dot(
        placement.T, returned_rows, preferred_element_type=jnp.float32
    )
    return (base_projection_output + adapter_row_output).astype(jnp.bfloat16)


def solution(mesh):
    in_specs = (
        P("wide", "tensor"),
        P(None, "tensor"),
        P("tensor", "wide", None),
        P("wide", None, "tensor"),
        P("wide"),
        P(),
    )
    out_specs = P("wide", "tensor")
    return jax.shard_map(body, mesh=mesh, in_specs=in_specs, out_specs=out_specs, check_vma=False)
```

```python
import jax
import jax.numpy as jnp
from jax import lax
from jax.sharding import PartitionSpec as P


def body(
    tokens,
    key_value_weight,
    adapter_down_maps,
    adapter_up_maps,
    adapter_per_row,
    adapter_storage_slot,
):
    row_count, feature_portion = tokens.shape
    wide_count = lax.axis_size("wide")
    tensor_count = lax.axis_size("tensor")
    capacity = 2 * row_count // wide_count
    present_adapters = adapter_down_maps.shape[1]
    rank_dimension = adapter_down_maps.shape[2]
    column_portion = key_value_weight.shape[1]
    total_adapters = adapter_storage_slot.shape[0]
    slot_count = wide_count * capacity
    lane = 128
    info_rows = 8

    gathered = lax.all_gather(tokens, "tensor", axis=1, tiled=True)
    base_projection_output = jnp.dot(
        gathered, key_value_weight, preferred_element_type=jnp.float32
    )

    adapter_match = adapter_per_row[:, None] == jnp.arange(total_adapters, dtype=jnp.int32)[None, :]
    storage_position = jnp.sum(jnp.where(adapter_match, adapter_storage_slot[None, :], 0), axis=1)
    owner_index = storage_position // present_adapters
    local_index = storage_position % present_adapters

    owner_onehot = (
        owner_index[:, None] == jnp.arange(wide_count, dtype=jnp.int32)[None, :]
    ).astype(jnp.float32)
    row_iota = jnp.arange(row_count, dtype=jnp.int32)
    strictly_before = (row_iota[:, None] > row_iota[None, :]).astype(jnp.float32)
    earlier = jnp.dot(strictly_before, owner_onehot, preferred_element_type=jnp.float32)
    rank_in_owner = jnp.sum(earlier * owner_onehot, axis=1).astype(jnp.int32)
    destination = owner_index * capacity + rank_in_owner

    placement = (
        jnp.arange(slot_count, dtype=jnp.int32)[:, None] == destination[None, :]
    ).astype(jnp.bfloat16)

    lane_tiles = feature_portion // lane
    local_code = jnp.broadcast_to(
        (local_index + 1).astype(jnp.bfloat16)[:, None], (row_count, lane)
    )
    pieces = []
    for tile in range(lane_tiles):
        placed = jnp.dot(
            placement, tokens[:, tile * lane : (tile + 1) * lane],
            preferred_element_type=jnp.float32,
        ).astype(jnp.bfloat16)
        pieces.append(placed.reshape(wide_count, capacity, lane))
    placed_code = jnp.dot(placement, local_code, preferred_element_type=jnp.float32)
    slot_code = placed_code[:, 0].astype(jnp.bfloat16).reshape(wide_count, 1, capacity)
    pieces.append(jnp.pad(slot_code, ((0, 0), (0, info_rows - 1), (0, lane - capacity))))
    send_block = jnp.concatenate(pieces, axis=1)

    got_block = lax.all_to_all(send_block, "wide", split_axis=0, concat_axis=0, tiled=True)
    flat_rows = jnp.concatenate(
        [
            got_block[:, tile * capacity : (tile + 1) * capacity, :].reshape(slot_count, lane)
            for tile in range(lane_tiles)
        ],
        axis=1,
    )
    got_code = (
        got_block[:, lane_tiles * capacity, :capacity].reshape(slot_count).astype(jnp.int32)
    )
    selected = (
        got_code[:, None] == jnp.arange(1, present_adapters + 1, dtype=jnp.int32)[None, :]
    )[:, :, None]

    down_matrix = adapter_down_maps.reshape(feature_portion, present_adapters * rank_dimension)
    all_ranks = jnp.dot(flat_rows, down_matrix, preferred_element_type=jnp.float32)
    all_ranks = all_ranks.reshape(slot_count, present_adapters, rank_dimension)
    partial_value = jnp.sum(jnp.where(selected, all_ranks, 0.0), axis=1)
    core = lax.axis_index("tensor") % 2
    chip_count = tensor_count // 2
    chip_groups = [list(range(c, tensor_count, 2)) for c in range(2)]
    pair_swap = [(i, i ^ 1) for i in range(tensor_count)]
    half = slot_count // 2
    low_half, high_half = partial_value[:half], partial_value[half:]
    keep = jnp.where(core == 1, high_half, low_half)
    send = jnp.where(core == 1, low_half, high_half)
    pair_sum = keep + lax.ppermute(send, "tensor", pair_swap)
    slot_blocks = pair_sum.reshape(chip_count, half // chip_count, rank_dimension)
    gathered_blocks = lax.all_to_all(
        slot_blocks, "tensor", split_axis=0, concat_axis=0, tiled=True,
        axis_index_groups=chip_groups,
    )
    own_sum = jnp.sum(gathered_blocks, axis=0).astype(jnp.bfloat16)
    spread = jnp.broadcast_to(own_sum[None], (chip_count,) + own_sum.shape)
    half_rows = lax.all_to_all(
        spread, "tensor", split_axis=0, concat_axis=0, tiled=True,
        axis_index_groups=chip_groups,
    ).reshape(half, rank_dimension)
    other_rows = lax.ppermute(half_rows, "tensor", pair_swap)
    reduced_rows = jnp.where(
        core == 1,
        jnp.concatenate([other_rows, half_rows], axis=0),
        jnp.concatenate([half_rows, other_rows], axis=0),
    )

    expanded_rows = jnp.where(
        selected, reduced_rows[:, None, :], jnp.zeros((), jnp.bfloat16)
    ).reshape(slot_count, present_adapters * rank_dimension)
    up_matrix = adapter_up_maps.reshape(present_adapters * rank_dimension, column_portion)
    adapter_correction = jnp.dot(
        expanded_rows, up_matrix, preferred_element_type=jnp.float32
    ).astype(jnp.bfloat16)
    adapter_correction = adapter_correction.reshape(wide_count, capacity, column_portion)
    returned_rows = lax.all_to_all(
        adapter_correction, "wide", split_axis=0, concat_axis=0, tiled=True
    )
    returned_rows = returned_rows.reshape(slot_count, column_portion)
    adapter_row_output = jnp.dot(
        placement.T, returned_rows, preferred_element_type=jnp.float32
    )
    return (base_projection_output + adapter_row_output).astype(jnp.bfloat16)


def solution(mesh):
    in_specs = (
        P("wide", "tensor"),
        P(None, "tensor"),
        P("tensor", "wide", None),
        P("wide", None, "tensor"),
        P("wide"),
        P(),
    )
    out_specs = P("wide", "tensor")
    return jax.shard_map(body, mesh=mesh, in_specs=in_specs, out_specs=out_specs, check_vma=False)
```

```python
import jax
import jax.numpy as jnp
from jax import lax
from jax.sharding import PartitionSpec as P


def body(
    tokens,
    key_value_weight,
    adapter_down_maps,
    adapter_up_maps,
    adapter_per_row,
    adapter_storage_slot,
):
    row_count, feature_portion = tokens.shape
    wide_count = lax.axis_size("wide")
    tensor_count = lax.axis_size("tensor")
    capacity = 2 * row_count // wide_count
    present_adapters = adapter_down_maps.shape[1]
    rank_dimension = adapter_down_maps.shape[2]
    column_portion = key_value_weight.shape[1]
    total_adapters = adapter_storage_slot.shape[0]
    slot_count = wide_count * capacity
    lane = 128
    info_rows = 8

    gathered = lax.all_gather(tokens, "tensor", axis=1, tiled=True)
    base_projection_output = jnp.dot(
        gathered, key_value_weight, preferred_element_type=jnp.float32
    )

    adapter_match = adapter_per_row[:, None] == jnp.arange(total_adapters, dtype=jnp.int32)[None, :]
    storage_position = jnp.sum(jnp.where(adapter_match, adapter_storage_slot[None, :], 0), axis=1)
    owner_index = storage_position // present_adapters
    local_index = storage_position % present_adapters

    owner_onehot = (
        owner_index[:, None] == jnp.arange(wide_count, dtype=jnp.int32)[None, :]
    ).astype(jnp.float32)
    row_iota = jnp.arange(row_count, dtype=jnp.int32)
    strictly_before = (row_iota[:, None] > row_iota[None, :]).astype(jnp.float32)
    earlier = jnp.dot(strictly_before, owner_onehot, preferred_element_type=jnp.float32)
    rank_in_owner = jnp.sum(earlier * owner_onehot, axis=1).astype(jnp.int32)
    destination = owner_index * capacity + rank_in_owner

    placement = (
        jnp.arange(slot_count, dtype=jnp.int32)[:, None] == destination[None, :]
    ).astype(jnp.bfloat16)

    lane_tiles = feature_portion // lane
    local_code = jnp.broadcast_to(
        (local_index + 1).astype(jnp.bfloat16)[:, None], (row_count, lane)
    )
    placement_blocks = placement.reshape(wide_count, capacity, row_count)
    token_tiles = tokens.reshape(row_count, lane_tiles, lane)
    placed = jnp.einsum(
        "dcr,rjl->djcl", placement_blocks, token_tiles, preferred_element_type=jnp.float32
    ).astype(jnp.bfloat16)
    pieces = [placed.reshape(wide_count, lane_tiles * capacity, lane)]
    placed_code = jnp.dot(placement, local_code, preferred_element_type=jnp.float32)
    slot_code = placed_code[:, 0].astype(jnp.bfloat16).reshape(wide_count, 1, capacity)
    pieces.append(jnp.pad(slot_code, ((0, 0), (0, info_rows - 1), (0, lane - capacity))))
    send_block = jnp.concatenate(pieces, axis=1)

    got_block = lax.all_to_all(send_block, "wide", split_axis=0, concat_axis=0, tiled=True)
    flat_rows = jnp.concatenate(
        [
            got_block[:, tile * capacity : (tile + 1) * capacity, :].reshape(slot_count, lane)
            for tile in range(lane_tiles)
        ],
        axis=1,
    )
    got_code = (
        got_block[:, lane_tiles * capacity, :capacity].reshape(slot_count).astype(jnp.int32)
    )
    selected = (
        got_code[:, None] == jnp.arange(1, present_adapters + 1, dtype=jnp.int32)[None, :]
    )[:, :, None]

    down_matrix = adapter_down_maps.reshape(feature_portion, present_adapters * rank_dimension)
    all_ranks = jnp.dot(flat_rows, down_matrix, preferred_element_type=jnp.float32)
    all_ranks = all_ranks.reshape(slot_count, present_adapters, rank_dimension)
    partial_value = jnp.sum(jnp.where(selected, all_ranks, 0.0), axis=1)
    slot_blocks = partial_value.reshape(tensor_count, slot_count // tensor_count, rank_dimension)
    gathered_blocks = lax.all_to_all(slot_blocks, "tensor", split_axis=0, concat_axis=0, tiled=True)
    own_sum = jnp.sum(gathered_blocks, axis=0).astype(jnp.bfloat16)
    spread = jnp.broadcast_to(own_sum[None], (tensor_count,) + own_sum.shape)
    reduced_rows = lax.all_to_all(spread, "tensor", split_axis=0, concat_axis=0, tiled=True)
    reduced_rows = reduced_rows.reshape(slot_count, rank_dimension)

    expanded_rows = jnp.where(
        selected, reduced_rows[:, None, :], jnp.zeros((), jnp.bfloat16)
    ).reshape(slot_count, present_adapters * rank_dimension)
    up_matrix = adapter_up_maps.reshape(present_adapters * rank_dimension, column_portion)
    adapter_correction = jnp.dot(
        expanded_rows, up_matrix, preferred_element_type=jnp.float32
    ).astype(jnp.bfloat16)
    adapter_correction = adapter_correction.reshape(wide_count, capacity, column_portion)
    returned_rows = lax.all_to_all(
        adapter_correction, "wide", split_axis=0, concat_axis=0, tiled=True
    )
    returned_rows = returned_rows.reshape(slot_count, column_portion)
    adapter_row_output = jnp.dot(
        placement.T, returned_rows, preferred_element_type=jnp.float32
    )
    return (base_projection_output + adapter_row_output).astype(jnp.bfloat16)


def solution(mesh):
    in_specs = (
        P("wide", "tensor"),
        P(None, "tensor"),
        P("tensor", "wide", None),
        P("wide", None, "tensor"),
        P("wide"),
        P(),
    )
    out_specs = P("wide", "tensor")
    return jax.shard_map(body, mesh=mesh, in_specs=in_specs, out_specs=out_specs, check_vma=False)
```

```python
import jax
import jax.numpy as jnp
from jax import lax
from jax.sharding import PartitionSpec as P


def body(
    tokens,
    key_value_weight,
    adapter_down_maps,
    adapter_up_maps,
    adapter_per_row,
    adapter_storage_slot,
):
    row_count, feature_portion = tokens.shape
    wide_count = lax.axis_size("wide")
    tensor_count = lax.axis_size("tensor")
    capacity = 2 * row_count // wide_count
    present_adapters = adapter_down_maps.shape[1]
    rank_dimension = adapter_down_maps.shape[2]
    column_portion = key_value_weight.shape[1]
    total_adapters = adapter_storage_slot.shape[0]
    slot_count = wide_count * capacity
    lane = 128
    info_rows = 8

    gathered = lax.all_gather(tokens, "tensor", axis=1, tiled=True)
    base_projection_output = jnp.dot(
        gathered, key_value_weight, preferred_element_type=jnp.float32
    )

    adapter_match = adapter_per_row[:, None] == jnp.arange(total_adapters, dtype=jnp.int32)[None, :]
    storage_position = jnp.sum(jnp.where(adapter_match, adapter_storage_slot[None, :], 0), axis=1)
    owner_index = storage_position // present_adapters
    local_index = storage_position % present_adapters

    owner_onehot = (
        owner_index[:, None] == jnp.arange(wide_count, dtype=jnp.int32)[None, :]
    ).astype(jnp.float32)
    row_iota = jnp.arange(row_count, dtype=jnp.int32)
    strictly_before = (row_iota[:, None] > row_iota[None, :]).astype(jnp.float32)
    earlier = jnp.dot(strictly_before, owner_onehot, preferred_element_type=jnp.float32)
    rank_in_owner = jnp.sum(earlier * owner_onehot, axis=1).astype(jnp.int32)
    destination = owner_index * capacity + rank_in_owner

    placement = (
        jnp.arange(slot_count, dtype=jnp.int32)[:, None] == destination[None, :]
    ).astype(jnp.bfloat16)

    lane_tiles = feature_portion // lane
    local_code = jnp.broadcast_to(
        (local_index + 1).astype(jnp.bfloat16)[:, None], (row_count, lane)
    )
    placement_blocks = placement.reshape(wide_count, capacity, row_count)
    token_tiles = tokens.reshape(row_count, lane_tiles, lane)
    placed = jnp.einsum(
        "dcr,rjl->djcl", placement_blocks, token_tiles, preferred_element_type=jnp.float32
    ).astype(jnp.bfloat16)
    pieces = [placed.reshape(wide_count, lane_tiles * capacity, lane)]
    placed_code = jnp.dot(placement, local_code, preferred_element_type=jnp.float32)
    slot_code = placed_code[:, 0].astype(jnp.bfloat16).reshape(wide_count, 1, capacity)
    pieces.append(jnp.pad(slot_code, ((0, 0), (0, info_rows - 1), (0, lane - capacity))))
    send_block = jnp.concatenate(pieces, axis=1)

    got_block = lax.all_to_all(send_block, "wide", split_axis=0, concat_axis=0, tiled=True)
    flat_rows = jnp.concatenate(
        [
            got_block[:, tile * capacity : (tile + 1) * capacity, :].reshape(slot_count, lane)
            for tile in range(lane_tiles)
        ],
        axis=1,
    )
    got_code = (
        got_block[:, lane_tiles * capacity, :capacity].reshape(slot_count).astype(jnp.int32)
    )
    selected = (
        got_code[:, None] == jnp.arange(1, present_adapters + 1, dtype=jnp.int32)[None, :]
    )[:, :, None]

    down_matrix = adapter_down_maps.reshape(feature_portion, present_adapters * rank_dimension)
    all_ranks = jnp.dot(flat_rows, down_matrix, preferred_element_type=jnp.float32)
    all_ranks = all_ranks.reshape(slot_count, present_adapters, rank_dimension)
    partial_value = jnp.sum(jnp.where(selected, all_ranks, 0.0), axis=1)
    core = lax.axis_index("tensor") % 2
    chip_count = tensor_count // 2
    chip_groups = [list(range(c, tensor_count, 2)) for c in range(2)]
    pair_swap = [(i, i ^ 1) for i in range(tensor_count)]
    half = slot_count // 2
    low_half, high_half = partial_value[:half], partial_value[half:]
    keep = jnp.where(core == 1, high_half, low_half)
    send = jnp.where(core == 1, low_half, high_half)
    pair_sum = keep + lax.ppermute(send, "tensor", pair_swap)
    slot_blocks = pair_sum.reshape(chip_count, half // chip_count, rank_dimension)
    gathered_blocks = lax.all_to_all(
        slot_blocks, "tensor", split_axis=0, concat_axis=0, tiled=True,
        axis_index_groups=chip_groups,
    )
    own_sum = jnp.sum(gathered_blocks, axis=0).astype(jnp.bfloat16)
    spread = jnp.broadcast_to(own_sum[None], (chip_count,) + own_sum.shape)
    half_rows = lax.all_to_all(
        spread, "tensor", split_axis=0, concat_axis=0, tiled=True,
        axis_index_groups=chip_groups,
    ).reshape(half, rank_dimension)
    other_rows = lax.ppermute(half_rows, "tensor", pair_swap)
    reduced_rows = jnp.where(
        core == 1,
        jnp.concatenate([other_rows, half_rows], axis=0),
        jnp.concatenate([half_rows, other_rows], axis=0),
    )

    expanded_rows = jnp.where(
        selected, reduced_rows[:, None, :], jnp.zeros((), jnp.bfloat16)
    ).reshape(slot_count, present_adapters * rank_dimension)
    up_matrix = adapter_up_maps.reshape(present_adapters * rank_dimension, column_portion)
    adapter_correction = jnp.dot(
        expanded_rows, up_matrix, preferred_element_type=jnp.float32
    ).astype(jnp.bfloat16)
    adapter_correction = adapter_correction.reshape(wide_count, capacity, column_portion)
    returned_rows = lax.all_to_all(
        adapter_correction, "wide", split_axis=0, concat_axis=0, tiled=True
    )
    returned_rows = returned_rows.reshape(slot_count, column_portion)
    adapter_row_output = jnp.dot(
        placement.T, returned_rows, preferred_element_type=jnp.float32
    )
    return (base_projection_output + adapter_row_output).astype(jnp.bfloat16)


def solution(mesh):
    in_specs = (
        P("wide", "tensor"),
        P(None, "tensor"),
        P("tensor", "wide", None),
        P("wide", None, "tensor"),
        P("wide"),
        P(),
    )
    out_specs = P("wide", "tensor")
    return jax.shard_map(body, mesh=mesh, in_specs=in_specs, out_specs=out_specs, check_vma=False)
```

```python
import jax
import jax.numpy as jnp
from jax import lax
from jax.sharding import PartitionSpec as P


def body(
    tokens,
    key_value_weight,
    adapter_down_maps,
    adapter_up_maps,
    adapter_per_row,
    adapter_storage_slot,
):
    row_count, feature_portion = tokens.shape
    wide_count = lax.axis_size("wide")
    tensor_count = lax.axis_size("tensor")
    capacity = 2 * row_count // wide_count
    present_adapters = adapter_down_maps.shape[1]
    rank_dimension = adapter_down_maps.shape[2]
    column_portion = key_value_weight.shape[1]
    total_adapters = adapter_storage_slot.shape[0]
    slot_count = wide_count * capacity
    lane = 128
    info_rows = 8

    gathered = lax.all_gather(tokens, "tensor", axis=1, tiled=True)
    base_projection_output = jnp.dot(
        gathered, key_value_weight, preferred_element_type=jnp.float32
    )

    adapter_match = adapter_per_row[:, None] == jnp.arange(total_adapters, dtype=jnp.int32)[None, :]
    storage_position = jnp.sum(jnp.where(adapter_match, adapter_storage_slot[None, :], 0), axis=1)
    owner_index = storage_position // present_adapters
    local_index = storage_position % present_adapters

    owner_onehot = (
        owner_index[:, None] == jnp.arange(wide_count, dtype=jnp.int32)[None, :]
    ).astype(jnp.float32)
    row_iota = jnp.arange(row_count, dtype=jnp.int32)
    strictly_before = (row_iota[:, None] > row_iota[None, :]).astype(jnp.float32)
    earlier = jnp.dot(strictly_before, owner_onehot, preferred_element_type=jnp.float32)
    rank_in_owner = jnp.sum(earlier * owner_onehot, axis=1).astype(jnp.int32)
    destination = owner_index * capacity + rank_in_owner

    placement = (
        jnp.arange(slot_count, dtype=jnp.int32)[:, None] == destination[None, :]
    ).astype(jnp.bfloat16)

    lane_tiles = feature_portion // lane
    local_code = jnp.broadcast_to(
        (local_index + 1).astype(jnp.bfloat16)[:, None], (row_count, lane)
    )
    placement_blocks = placement.reshape(wide_count, capacity, row_count)
    token_tiles = tokens.reshape(row_count, lane_tiles, lane)
    placed = jnp.einsum(
        "dcr,rjl->djcl", placement_blocks, token_tiles, preferred_element_type=jnp.float32
    ).astype(jnp.bfloat16)
    pieces = [placed.reshape(wide_count, lane_tiles * capacity, lane)]
    placed_code = jnp.dot(placement, local_code, preferred_element_type=jnp.float32)
    slot_code = placed_code[:, 0].astype(jnp.bfloat16).reshape(wide_count, 1, capacity)
    pieces.append(jnp.pad(slot_code, ((0, 0), (0, info_rows - 1), (0, lane - capacity))))
    send_block = jnp.concatenate(pieces, axis=1)

    got_block = lax.all_to_all(send_block, "wide", split_axis=0, concat_axis=0, tiled=True)
    flat_rows = jnp.concatenate(
        [
            got_block[:, tile * capacity : (tile + 1) * capacity, :].reshape(slot_count, lane)
            for tile in range(lane_tiles)
        ],
        axis=1,
    )
    got_code = (
        got_block[:, lane_tiles * capacity, :capacity].reshape(slot_count).astype(jnp.int32)
    )
    selected = (
        got_code[:, None] == jnp.arange(1, present_adapters + 1, dtype=jnp.int32)[None, :]
    )[:, :, None]

    down_matrix = adapter_down_maps.reshape(feature_portion, present_adapters * rank_dimension)
    all_ranks = jnp.dot(flat_rows, down_matrix, preferred_element_type=jnp.float32)
    all_ranks = all_ranks.reshape(slot_count, present_adapters, rank_dimension)
    partial_value = jnp.sum(jnp.where(selected, all_ranks, 0.0), axis=1)
    block_rows = slot_count // tensor_count
    dense_shape = (tensor_count, 8, block_rows * rank_dimension // 8)
    slot_blocks = partial_value.reshape(dense_shape)
    gathered_blocks = lax.all_to_all(slot_blocks, "tensor", split_axis=0, concat_axis=0, tiled=True)
    own_sum = jnp.sum(gathered_blocks, axis=0).astype(jnp.bfloat16)
    spread_shape = (tensor_count, 16, block_rows * rank_dimension // 16)
    spread = jnp.broadcast_to(own_sum.reshape(spread_shape[1:])[None], spread_shape)
    reduced_rows = lax.all_to_all(spread, "tensor", split_axis=0, concat_axis=0, tiled=True)
    reduced_rows = reduced_rows.reshape(slot_count, rank_dimension)

    expanded_rows = jnp.where(
        selected, reduced_rows[:, None, :], jnp.zeros((), jnp.bfloat16)
    ).reshape(slot_count, present_adapters * rank_dimension)
    up_matrix = adapter_up_maps.reshape(present_adapters * rank_dimension, column_portion)
    adapter_correction = jnp.dot(
        expanded_rows, up_matrix, preferred_element_type=jnp.float32
    ).astype(jnp.bfloat16)
    adapter_correction = adapter_correction.reshape(wide_count, capacity, column_portion)
    returned_rows = lax.all_to_all(
        adapter_correction, "wide", split_axis=0, concat_axis=0, tiled=True
    )
    returned_rows = returned_rows.reshape(slot_count, column_portion)
    adapter_row_output = jnp.dot(
        placement.T, returned_rows, preferred_element_type=jnp.float32
    )
    return (base_projection_output + adapter_row_output).astype(jnp.bfloat16)


def solution(mesh):
    in_specs = (
        P("wide", "tensor"),
        P(None, "tensor"),
        P("tensor", "wide", None),
        P("wide", None, "tensor"),
        P("wide"),
        P(),
    )
    out_specs = P("wide", "tensor")
    return jax.shard_map(body, mesh=mesh, in_specs=in_specs, out_specs=out_specs, check_vma=False)
```

```python
import jax
import jax.numpy as jnp
from jax import lax
from jax.sharding import PartitionSpec as P


def body(
    tokens,
    key_value_weight,
    adapter_down_maps,
    adapter_up_maps,
    adapter_per_row,
    adapter_storage_slot,
):
    row_count, feature_portion = tokens.shape
    wide_count = lax.axis_size("wide")
    tensor_count = lax.axis_size("tensor")
    capacity = 2 * row_count // wide_count
    present_adapters = adapter_down_maps.shape[1]
    rank_dimension = adapter_down_maps.shape[2]
    column_portion = key_value_weight.shape[1]
    total_adapters = adapter_storage_slot.shape[0]
    slot_count = wide_count * capacity
    lane = 128
    info_rows = 8

    gathered = lax.all_gather(tokens, "tensor", axis=1, tiled=True)
    base_projection_output = jnp.dot(
        gathered, key_value_weight, preferred_element_type=jnp.float32
    )

    adapter_match = (
        adapter_per_row[:, None] == jnp.arange(total_adapters, dtype=jnp.int32)[None, :]
    ).astype(jnp.bfloat16)
    slot_parts = jnp.stack(
        [adapter_storage_slot // present_adapters, adapter_storage_slot % present_adapters], axis=1
    ).astype(jnp.bfloat16)
    picked = jnp.dot(adapter_match, slot_parts, preferred_element_type=jnp.float32)
    owner_index = picked[:, 0].astype(jnp.int32)
    local_index = picked[:, 1].astype(jnp.int32)

    owner_onehot = (
        owner_index[:, None] == jnp.arange(wide_count, dtype=jnp.int32)[None, :]
    ).astype(jnp.float32)
    row_iota = jnp.arange(row_count, dtype=jnp.int32)
    strictly_before = (row_iota[:, None] > row_iota[None, :]).astype(jnp.float32)
    earlier = jnp.dot(strictly_before, owner_onehot, preferred_element_type=jnp.float32)
    rank_in_owner = jnp.sum(earlier * owner_onehot, axis=1).astype(jnp.int32)
    destination = owner_index * capacity + rank_in_owner

    placement = (
        jnp.arange(slot_count, dtype=jnp.int32)[:, None] == destination[None, :]
    ).astype(jnp.bfloat16)

    lane_tiles = feature_portion // lane
    local_code = jnp.broadcast_to(
        (local_index + 1).astype(jnp.bfloat16)[:, None], (row_count, lane)
    )
    placement_blocks = placement.reshape(wide_count, capacity, row_count)
    token_tiles = tokens.reshape(row_count, lane_tiles, lane)
    placed = jnp.einsum(
        "dcr,rjl->djcl", placement_blocks, token_tiles, preferred_element_type=jnp.float32
    ).astype(jnp.bfloat16)
    pieces = [placed.reshape(wide_count, lane_tiles * capacity, lane)]
    placed_code = jnp.dot(placement, local_code, preferred_element_type=jnp.float32)
    slot_code = placed_code[:, 0].astype(jnp.bfloat16).reshape(wide_count, 1, capacity)
    pieces.append(jnp.pad(slot_code, ((0, 0), (0, info_rows - 1), (0, lane - capacity))))
    send_block = jnp.concatenate(pieces, axis=1)

    got_block = lax.all_to_all(send_block, "wide", split_axis=0, concat_axis=0, tiled=True)
    flat_rows = jnp.concatenate(
        [
            got_block[:, tile * capacity : (tile + 1) * capacity, :].reshape(slot_count, lane)
            for tile in range(lane_tiles)
        ],
        axis=1,
    )
    got_code = (
        got_block[:, lane_tiles * capacity, :capacity].reshape(slot_count).astype(jnp.int32)
    )
    selected = (
        got_code[:, None] == jnp.arange(1, present_adapters + 1, dtype=jnp.int32)[None, :]
    )[:, :, None]

    down_matrix = adapter_down_maps.reshape(feature_portion, present_adapters * rank_dimension)
    all_ranks = jnp.dot(flat_rows, down_matrix, preferred_element_type=jnp.float32)
    all_ranks = all_ranks.reshape(slot_count, present_adapters, rank_dimension)
    partial_value = jnp.sum(jnp.where(selected, all_ranks, 0.0), axis=1)
    block_rows = slot_count // tensor_count
    dense_shape = (tensor_count, 8, block_rows * rank_dimension // 8)
    slot_blocks = partial_value.reshape(dense_shape)
    gathered_blocks = lax.all_to_all(slot_blocks, "tensor", split_axis=0, concat_axis=0, tiled=True)
    own_sum = jnp.sum(gathered_blocks, axis=0).astype(jnp.bfloat16)
    spread_shape = (tensor_count, 16, block_rows * rank_dimension // 16)
    spread = jnp.broadcast_to(own_sum.reshape(spread_shape[1:])[None], spread_shape)
    reduced_rows = lax.all_to_all(spread, "tensor", split_axis=0, concat_axis=0, tiled=True)
    reduced_rows = reduced_rows.reshape(slot_count, rank_dimension)

    expanded_rows = jnp.where(
        selected, reduced_rows[:, None, :], jnp.zeros((), jnp.bfloat16)
    ).reshape(slot_count, present_adapters * rank_dimension)
    up_matrix = adapter_up_maps.reshape(present_adapters * rank_dimension, column_portion)
    adapter_correction = jnp.dot(
        expanded_rows, up_matrix, preferred_element_type=jnp.float32
    ).astype(jnp.bfloat16)
    adapter_correction = adapter_correction.reshape(wide_count, capacity, column_portion)
    returned_rows = lax.all_to_all(
        adapter_correction, "wide", split_axis=0, concat_axis=0, tiled=True
    )
    returned_rows = returned_rows.reshape(slot_count, column_portion)
    adapter_row_output = jnp.dot(
        placement.T, returned_rows, preferred_element_type=jnp.float32
    )
    return (base_projection_output + adapter_row_output).astype(jnp.bfloat16)


def solution(mesh):
    in_specs = (
        P("wide", "tensor"),
        P(None, "tensor"),
        P("tensor", "wide", None),
        P("wide", None, "tensor"),
        P("wide"),
        P(),
    )
    out_specs = P("wide", "tensor")
    return jax.shard_map(body, mesh=mesh, in_specs=in_specs, out_specs=out_specs, check_vma=False)
```

```python
import jax
import jax.numpy as jnp
from jax import lax
from jax.sharding import PartitionSpec as P


def body(
    tokens,
    key_value_weight,
    adapter_down_maps,
    adapter_up_maps,
    adapter_per_row,
    adapter_storage_slot,
):
    row_count, feature_portion = tokens.shape
    wide_count = lax.axis_size("wide")
    tensor_count = lax.axis_size("tensor")
    capacity = 2 * row_count // wide_count
    present_adapters = adapter_down_maps.shape[1]
    rank_dimension = adapter_down_maps.shape[2]
    column_portion = key_value_weight.shape[1]
    total_adapters = adapter_storage_slot.shape[0]
    slot_count = wide_count * capacity
    lane = 128
    info_rows = 8

    gathered = lax.all_gather(tokens, "tensor", axis=1, tiled=True)
    base_projection_output = jnp.dot(
        gathered, key_value_weight, preferred_element_type=jnp.float32
    )

    adapter_match = (
        adapter_per_row[:, None] == jnp.arange(total_adapters, dtype=jnp.int32)[None, :]
    ).astype(jnp.bfloat16)
    slot_parts = jnp.stack(
        [adapter_storage_slot // present_adapters, adapter_storage_slot % present_adapters], axis=1
    ).astype(jnp.bfloat16)
    picked = jnp.dot(adapter_match, slot_parts, preferred_element_type=jnp.float32)
    owner_index = picked[:, 0].astype(jnp.int32)
    local_index = picked[:, 1].astype(jnp.int32)

    owner_onehot = (
        owner_index[:, None] == jnp.arange(wide_count, dtype=jnp.int32)[None, :]
    ).astype(jnp.float32)
    row_iota = jnp.arange(row_count, dtype=jnp.int32)
    strictly_before = (row_iota[:, None] > row_iota[None, :]).astype(jnp.float32)
    earlier = jnp.dot(strictly_before, owner_onehot, preferred_element_type=jnp.float32)
    rank_in_owner = jnp.sum(earlier * owner_onehot, axis=1).astype(jnp.int32)
    destination = owner_index * capacity + rank_in_owner

    placement = (
        jnp.arange(slot_count, dtype=jnp.int32)[:, None] == destination[None, :]
    ).astype(jnp.bfloat16)

    lane_tiles = feature_portion // lane
    local_code = jnp.broadcast_to(
        (local_index + 1).astype(jnp.bfloat16)[:, None], (row_count, lane)
    )
    placement_blocks = placement.reshape(wide_count, capacity, row_count)
    token_tiles = tokens.reshape(row_count, lane_tiles, lane)
    placed = jnp.einsum(
        "dcr,rjl->djcl", placement_blocks, token_tiles, preferred_element_type=jnp.float32
    ).astype(jnp.bfloat16)
    pieces = [placed.reshape(wide_count, lane_tiles * capacity, lane)]
    placed_code = jnp.dot(placement, local_code, preferred_element_type=jnp.float32)
    slot_code = placed_code[:, 0].astype(jnp.bfloat16).reshape(wide_count, 1, capacity)
    pieces.append(jnp.pad(slot_code, ((0, 0), (0, info_rows - 1), (0, lane - capacity))))
    send_block = jnp.concatenate(pieces, axis=1)

    got_block = lax.all_to_all(send_block, "wide", split_axis=0, concat_axis=0, tiled=True)
    flat_rows = jnp.concatenate(
        [
            got_block[:, tile * capacity : (tile + 1) * capacity, :].reshape(slot_count, lane)
            for tile in range(lane_tiles)
        ],
        axis=1,
    )
    got_code = (
        got_block[:, lane_tiles * capacity, :capacity].reshape(slot_count).astype(jnp.int32)
    )
    selected = (
        got_code[:, None] == jnp.arange(1, present_adapters + 1, dtype=jnp.int32)[None, :]
    )[:, :, None]

    down_matrix = adapter_down_maps.reshape(feature_portion, present_adapters * rank_dimension)
    all_ranks = jnp.dot(flat_rows, down_matrix, preferred_element_type=jnp.float32)
    all_ranks = all_ranks.reshape(slot_count, present_adapters, rank_dimension)
    partial_value = jnp.sum(jnp.where(selected, all_ranks, 0.0), axis=1)
    block_rows = slot_count // tensor_count
    slot_blocks = partial_value.reshape(tensor_count, block_rows, rank_dimension)
    gathered_blocks = lax.all_to_all(slot_blocks, "tensor", split_axis=0, concat_axis=0, tiled=True)
    own_sum = jnp.sum(gathered_blocks, axis=0).astype(jnp.bfloat16)
    spread_shape = (tensor_count, 16, block_rows * rank_dimension // 16)
    spread = jnp.broadcast_to(own_sum.reshape(spread_shape[1:])[None], spread_shape)
    reduced_rows = lax.all_to_all(spread, "tensor", split_axis=0, concat_axis=0, tiled=True)
    reduced_rows = reduced_rows.reshape(slot_count, rank_dimension)

    expanded_rows = jnp.where(
        selected, reduced_rows[:, None, :], jnp.zeros((), jnp.bfloat16)
    ).reshape(slot_count, present_adapters * rank_dimension)
    up_matrix = adapter_up_maps.reshape(present_adapters * rank_dimension, column_portion)
    adapter_correction = jnp.dot(
        expanded_rows, up_matrix, preferred_element_type=jnp.float32
    ).astype(jnp.bfloat16)
    adapter_correction = adapter_correction.reshape(wide_count, capacity, column_portion)
    returned_rows = lax.all_to_all(
        adapter_correction, "wide", split_axis=0, concat_axis=0, tiled=True
    )
    returned_rows = returned_rows.reshape(slot_count, column_portion)
    adapter_row_output = jnp.dot(
        placement.T, returned_rows, preferred_element_type=jnp.float32
    )
    return (base_projection_output + adapter_row_output).astype(jnp.bfloat16)


def solution(mesh):
    in_specs = (
        P("wide", "tensor"),
        P(None, "tensor"),
        P("tensor", "wide", None),
        P("wide", None, "tensor"),
        P("wide"),
        P(),
    )
    out_specs = P("wide", "tensor")
    return jax.shard_map(body, mesh=mesh, in_specs=in_specs, out_specs=out_specs, check_vma=False)
```

```python
import jax
import jax.numpy as jnp
from jax import lax
from jax.sharding import PartitionSpec as P


def body(
    tokens,
    key_value_weight,
    adapter_down_maps,
    adapter_up_maps,
    adapter_per_row,
    adapter_storage_slot,
):
    row_count, feature_portion = tokens.shape
    wide_count = lax.axis_size("wide")
    tensor_count = lax.axis_size("tensor")
    capacity = 2 * row_count // wide_count
    present_adapters = adapter_down_maps.shape[1]
    rank_dimension = adapter_down_maps.shape[2]
    column_portion = key_value_weight.shape[1]
    total_adapters = adapter_storage_slot.shape[0]
    slot_count = wide_count * capacity
    lane = 128
    info_rows = 8

    gathered = lax.all_gather(tokens, "tensor", axis=1, tiled=True)
    base_projection_output = jnp.dot(
        gathered, key_value_weight, preferred_element_type=jnp.float32
    )

    adapter_match = (
        adapter_per_row[:, None] == jnp.arange(total_adapters, dtype=jnp.int32)[None, :]
    ).astype(jnp.bfloat16)
    slot_parts = jnp.stack(
        [adapter_storage_slot // present_adapters, adapter_storage_slot % present_adapters], axis=1
    ).astype(jnp.bfloat16)
    picked = jnp.dot(adapter_match, slot_parts, preferred_element_type=jnp.float32)
    owner_index = picked[:, 0].astype(jnp.int32)
    local_index = picked[:, 1].astype(jnp.int32)

    owner_onehot = (
        owner_index[:, None] == jnp.arange(wide_count, dtype=jnp.int32)[None, :]
    ).astype(jnp.float32)
    row_iota = jnp.arange(row_count, dtype=jnp.int32)
    strictly_before = (row_iota[:, None] > row_iota[None, :]).astype(jnp.float32)
    earlier = jnp.dot(strictly_before, owner_onehot, preferred_element_type=jnp.float32)
    rank_in_owner = jnp.sum(earlier * owner_onehot, axis=1).astype(jnp.int32)
    destination = owner_index * capacity + rank_in_owner

    placement = (
        jnp.arange(slot_count, dtype=jnp.int32)[:, None] == destination[None, :]
    ).astype(jnp.bfloat16)

    lane_tiles = feature_portion // lane
    local_code = jnp.broadcast_to(
        (local_index + 1).astype(jnp.bfloat16)[:, None], (row_count, lane)
    )
    placement_blocks = placement.reshape(wide_count, capacity, row_count)
    token_tiles = tokens.reshape(row_count, lane_tiles, lane)
    placed = jnp.einsum(
        "dcr,rjl->djcl", placement_blocks, token_tiles, preferred_element_type=jnp.float32
    ).astype(jnp.bfloat16)
    pieces = [placed.reshape(wide_count, lane_tiles * capacity, lane)]
    placed_code = jnp.dot(placement, local_code, preferred_element_type=jnp.float32)
    slot_code = placed_code[:, 0].astype(jnp.bfloat16).reshape(wide_count, 1, capacity)
    pieces.append(jnp.pad(slot_code, ((0, 0), (0, info_rows - 1), (0, lane - capacity))))
    send_block = jnp.concatenate(pieces, axis=1)

    got_block = lax.all_to_all(send_block, "wide", split_axis=0, concat_axis=0, tiled=True)
    flat_rows = jnp.concatenate(
        [
            got_block[:, tile * capacity : (tile + 1) * capacity, :].reshape(slot_count, lane)
            for tile in range(lane_tiles)
        ],
        axis=1,
    )
    got_code = (
        got_block[:, lane_tiles * capacity, :capacity].reshape(slot_count).astype(jnp.int32)
    )
    selected = (
        got_code[:, None] == jnp.arange(1, present_adapters + 1, dtype=jnp.int32)[None, :]
    )[:, :, None]

    down_matrix = adapter_down_maps.reshape(feature_portion, present_adapters * rank_dimension)
    all_ranks = jnp.dot(flat_rows, down_matrix, preferred_element_type=jnp.float32)
    all_ranks = all_ranks.reshape(slot_count, present_adapters, rank_dimension)
    partial_value = jnp.sum(jnp.where(selected, all_ranks, 0.0), axis=1)
    block_rows = slot_count // tensor_count
    dense_shape = (tensor_count, 8, block_rows * rank_dimension // 8)
    slot_blocks = partial_value.reshape(dense_shape)
    gathered_blocks = lax.all_to_all(slot_blocks, "tensor", split_axis=0, concat_axis=0, tiled=True)
    own_sum = jnp.sum(gathered_blocks, axis=0).astype(jnp.bfloat16)
    spread_shape = (tensor_count, 16, block_rows * rank_dimension // 16)
    spread = jnp.broadcast_to(own_sum.reshape(spread_shape[1:])[None], spread_shape)
    reduced_rows = lax.all_to_all(spread, "tensor", split_axis=0, concat_axis=0, tiled=True)
    reduced_rows = reduced_rows.reshape(slot_count, rank_dimension)

    base_tie = (base_projection_output[0, 0] * 0.0).astype(jnp.bfloat16)
    expanded_rows = jnp.where(
        selected, reduced_rows[:, None, :] + base_tie, jnp.zeros((), jnp.bfloat16)
    ).reshape(slot_count, present_adapters * rank_dimension)
    up_matrix = adapter_up_maps.reshape(present_adapters * rank_dimension, column_portion)
    adapter_correction = jnp.dot(
        expanded_rows, up_matrix, preferred_element_type=jnp.float32
    ).astype(jnp.bfloat16)
    adapter_correction = adapter_correction.reshape(wide_count, capacity, column_portion)
    returned_rows = lax.all_to_all(
        adapter_correction, "wide", split_axis=0, concat_axis=0, tiled=True
    )
    returned_rows = returned_rows.reshape(slot_count, column_portion)
    adapter_row_output = jnp.dot(
        placement.T, returned_rows, preferred_element_type=jnp.float32
    )
    return (base_projection_output + adapter_row_output).astype(jnp.bfloat16)


def solution(mesh):
    in_specs = (
        P("wide", "tensor"),
        P(None, "tensor"),
        P("tensor", "wide", None),
        P("wide", None, "tensor"),
        P("wide"),
        P(),
    )
    out_specs = P("wide", "tensor")
    return jax.shard_map(body, mesh=mesh, in_specs=in_specs, out_specs=out_specs, check_vma=False)
```

```python
import jax
import jax.numpy as jnp
from jax import lax
from jax.sharding import PartitionSpec as P


def body(
    tokens,
    key_value_weight,
    adapter_down_maps,
    adapter_up_maps,
    adapter_per_row,
    adapter_storage_slot,
):
    row_count, feature_portion = tokens.shape
    wide_count = lax.axis_size("wide")
    tensor_count = lax.axis_size("tensor")
    capacity = 2 * row_count // wide_count
    present_adapters = adapter_down_maps.shape[1]
    rank_dimension = adapter_down_maps.shape[2]
    column_portion = key_value_weight.shape[1]
    total_adapters = adapter_storage_slot.shape[0]
    slot_count = wide_count * capacity
    lane = 128
    info_rows = 8

    gathered = lax.all_gather(tokens, "tensor", axis=1, tiled=True)
    base_projection_output = jnp.dot(
        gathered, key_value_weight, preferred_element_type=jnp.float32
    )

    adapter_match = (
        adapter_per_row[:, None] == jnp.arange(total_adapters, dtype=jnp.int32)[None, :]
    ).astype(jnp.bfloat16)
    slot_parts = jnp.stack(
        [adapter_storage_slot // present_adapters, adapter_storage_slot % present_adapters], axis=1
    ).astype(jnp.bfloat16)
    picked = jnp.dot(adapter_match, slot_parts, preferred_element_type=jnp.float32)
    owner_index = picked[:, 0].astype(jnp.int32)
    local_index = picked[:, 1].astype(jnp.int32)

    owner_onehot = (
        owner_index[:, None] == jnp.arange(wide_count, dtype=jnp.int32)[None, :]
    ).astype(jnp.float32)
    row_iota = jnp.arange(row_count, dtype=jnp.int32)
    strictly_before = (row_iota[:, None] > row_iota[None, :]).astype(jnp.float32)
    earlier = jnp.dot(strictly_before, owner_onehot, preferred_element_type=jnp.float32)
    rank_in_owner = jnp.sum(earlier * owner_onehot, axis=1).astype(jnp.int32)
    destination = owner_index * capacity + rank_in_owner

    placement = (
        jnp.arange(slot_count, dtype=jnp.int32)[:, None] == destination[None, :]
    ).astype(jnp.bfloat16)

    lane_tiles = feature_portion // lane
    local_code = jnp.broadcast_to(
        (local_index + 1).astype(jnp.bfloat16)[:, None], (row_count, lane)
    )
    placement_blocks = placement.reshape(wide_count, capacity, row_count)
    token_tiles = tokens.reshape(row_count, lane_tiles, lane)
    placed = jnp.einsum(
        "dcr,rjl->djcl", placement_blocks, token_tiles, preferred_element_type=jnp.float32
    ).astype(jnp.bfloat16)
    pieces = [placed.reshape(wide_count, lane_tiles * capacity, lane)]
    placed_code = jnp.dot(placement, local_code, preferred_element_type=jnp.float32)
    slot_code = placed_code[:, 0].astype(jnp.bfloat16).reshape(wide_count, 1, capacity)
    pieces.append(jnp.pad(slot_code, ((0, 0), (0, info_rows - 1), (0, lane - capacity))))
    send_block = jnp.concatenate(pieces, axis=1)

    got_block = lax.all_to_all(send_block, "wide", split_axis=0, concat_axis=0, tiled=True)
    flat_rows = jnp.concatenate(
        [
            got_block[:, tile * capacity : (tile + 1) * capacity, :].reshape(slot_count, lane)
            for tile in range(lane_tiles)
        ],
        axis=1,
    )
    got_code = (
        got_block[:, lane_tiles * capacity, :capacity].reshape(slot_count).astype(jnp.int32)
    )
    selected = (
        got_code[:, None] == jnp.arange(1, present_adapters + 1, dtype=jnp.int32)[None, :]
    )[:, :, None]

    down_matrix = adapter_down_maps.reshape(feature_portion, present_adapters * rank_dimension)
    all_ranks = jnp.dot(flat_rows, down_matrix, preferred_element_type=jnp.float32)
    all_ranks = all_ranks.reshape(slot_count, present_adapters, rank_dimension)
    partial_value = jnp.sum(jnp.where(selected, all_ranks, 0.0), axis=1)
    block_rows = slot_count // tensor_count
    dense_shape = (tensor_count, 8, block_rows * rank_dimension // 8)
    slot_blocks = partial_value.reshape(dense_shape)
    gathered_blocks = lax.all_to_all(slot_blocks, "tensor", split_axis=0, concat_axis=0, tiled=True)
    own_sum = jnp.sum(gathered_blocks, axis=0).astype(jnp.bfloat16)
    spread_shape = (tensor_count, 16, block_rows * rank_dimension // 16)
    spread = jnp.broadcast_to(own_sum.reshape(spread_shape[1:])[None], spread_shape)
    reduced_rows = lax.all_to_all(spread, "tensor", split_axis=0, concat_axis=0, tiled=True)
    reduced_rows = reduced_rows.reshape(slot_count, rank_dimension)

    base_tie = (base_projection_output[0, 0] * 0.0).astype(jnp.bfloat16)
    expanded_rows = jnp.where(
        selected, reduced_rows[:, None, :] + base_tie, jnp.zeros((), jnp.bfloat16)
    ).reshape(slot_count, present_adapters * rank_dimension)
    up_matrix = adapter_up_maps.reshape(present_adapters * rank_dimension, column_portion)
    adapter_correction = jnp.dot(
        expanded_rows, up_matrix, preferred_element_type=jnp.float32
    ).astype(jnp.bfloat16)
    adapter_correction = adapter_correction.reshape(wide_count, capacity // 2, 2 * column_portion)
    returned_rows = lax.all_to_all(
        adapter_correction, "wide", split_axis=0, concat_axis=0, tiled=True
    )
    returned_rows = returned_rows.reshape(slot_count, column_portion)
    adapter_row_output = jnp.dot(
        placement.T, returned_rows, preferred_element_type=jnp.float32
    )
    return (base_projection_output + adapter_row_output).astype(jnp.bfloat16)


def solution(mesh):
    in_specs = (
        P("wide", "tensor"),
        P(None, "tensor"),
        P("tensor", "wide", None),
        P("wide", None, "tensor"),
        P("wide"),
        P(),
    )
    out_specs = P("wide", "tensor")
    return jax.shard_map(body, mesh=mesh, in_specs=in_specs, out_specs=out_specs, check_vma=False)
```

```python
import jax
import jax.numpy as jnp
from jax import lax
from jax.sharding import PartitionSpec as P


def body(
    tokens,
    key_value_weight,
    adapter_down_maps,
    adapter_up_maps,
    adapter_per_row,
    adapter_storage_slot,
):
    row_count, feature_portion = tokens.shape
    wide_count = lax.axis_size("wide")
    tensor_count = lax.axis_size("tensor")
    capacity = 2 * row_count // wide_count
    present_adapters = adapter_down_maps.shape[1]
    rank_dimension = adapter_down_maps.shape[2]
    column_portion = key_value_weight.shape[1]
    total_adapters = adapter_storage_slot.shape[0]
    slot_count = wide_count * capacity
    lane = 128
    info_rows = 8

    gathered = lax.all_gather(tokens, "tensor", axis=1, tiled=True)
    base_projection_output = jnp.dot(
        gathered, key_value_weight, preferred_element_type=jnp.float32
    )

    adapter_match = (
        adapter_per_row[:, None] == jnp.arange(total_adapters, dtype=jnp.int32)[None, :]
    ).astype(jnp.bfloat16)
    slot_parts = jnp.stack(
        [adapter_storage_slot // present_adapters, adapter_storage_slot % present_adapters], axis=1
    ).astype(jnp.bfloat16)
    picked = jnp.dot(adapter_match, slot_parts, preferred_element_type=jnp.float32)
    owner_index = picked[:, 0].astype(jnp.int32)
    local_index = picked[:, 1].astype(jnp.int32)

    owner_onehot = (
        owner_index[:, None] == jnp.arange(wide_count, dtype=jnp.int32)[None, :]
    ).astype(jnp.float32)
    row_iota = jnp.arange(row_count, dtype=jnp.int32)
    strictly_before = (row_iota[:, None] > row_iota[None, :]).astype(jnp.float32)
    earlier = jnp.dot(strictly_before, owner_onehot, preferred_element_type=jnp.float32)
    rank_in_owner = jnp.sum(earlier * owner_onehot, axis=1).astype(jnp.int32)
    destination = owner_index * capacity + rank_in_owner

    placement = (
        jnp.arange(slot_count, dtype=jnp.int32)[:, None] == destination[None, :]
    ).astype(jnp.bfloat16)

    lane_tiles = feature_portion // lane
    local_code = jnp.broadcast_to(
        (local_index + 1).astype(jnp.bfloat16)[:, None], (row_count, lane)
    )
    placement_blocks = placement.reshape(wide_count, capacity, row_count)
    token_tiles = tokens.reshape(row_count, lane_tiles, lane)
    placed = jnp.einsum(
        "dcr,rjl->djcl", placement_blocks, token_tiles, preferred_element_type=jnp.float32
    ).astype(jnp.bfloat16)
    pieces = [placed.reshape(wide_count, lane_tiles * capacity, lane)]
    placed_code = jnp.dot(placement, local_code, preferred_element_type=jnp.float32)
    slot_code = placed_code[:, 0].astype(jnp.bfloat16).reshape(wide_count, 1, capacity)
    pieces.append(jnp.pad(slot_code, ((0, 0), (0, info_rows - 1), (0, lane - capacity))))
    send_block = jnp.concatenate(pieces, axis=1)

    got_block = lax.all_to_all(send_block, "wide", split_axis=0, concat_axis=0, tiled=True)
    flat_rows = jnp.concatenate(
        [
            got_block[:, tile * capacity : (tile + 1) * capacity, :].reshape(slot_count, lane)
            for tile in range(lane_tiles)
        ],
        axis=1,
    )
    got_code = (
        got_block[:, lane_tiles * capacity, :capacity].reshape(slot_count).astype(jnp.int32)
    )
    selected = (
        got_code[:, None] == jnp.arange(1, present_adapters + 1, dtype=jnp.int32)[None, :]
    )[:, :, None]

    down_matrix = adapter_down_maps.reshape(feature_portion, present_adapters * rank_dimension)
    all_ranks = jnp.dot(flat_rows, down_matrix, preferred_element_type=jnp.float32)
    all_ranks = all_ranks.reshape(slot_count, present_adapters, rank_dimension)
    partial_value = jnp.sum(jnp.where(selected, all_ranks, 0.0), axis=1)
    block_rows = slot_count // tensor_count
    dense_shape = (tensor_count, block_rows * rank_dimension // 128, 128)
    slot_blocks = partial_value.reshape(dense_shape)
    gathered_blocks = lax.all_to_all(slot_blocks, "tensor", split_axis=0, concat_axis=0, tiled=True)
    own_sum = jnp.sum(gathered_blocks, axis=0).astype(jnp.bfloat16)
    spread_shape = (tensor_count, 16, block_rows * rank_dimension // 16)
    spread = jnp.broadcast_to(own_sum.reshape(spread_shape[1:])[None], spread_shape)
    reduced_rows = lax.all_to_all(spread, "tensor", split_axis=0, concat_axis=0, tiled=True)
    reduced_rows = reduced_rows.reshape(slot_count, rank_dimension)

    base_tie = (base_projection_output[0, 0] * 0.0).astype(jnp.bfloat16)
    expanded_rows = jnp.where(
        selected, reduced_rows[:, None, :] + base_tie, jnp.zeros((), jnp.bfloat16)
    ).reshape(slot_count, present_adapters * rank_dimension)
    up_matrix = adapter_up_maps.reshape(present_adapters * rank_dimension, column_portion)
    adapter_correction = jnp.dot(
        expanded_rows, up_matrix, preferred_element_type=jnp.float32
    ).astype(jnp.bfloat16)
    adapter_correction = adapter_correction.reshape(wide_count, capacity, column_portion)
    returned_rows = lax.all_to_all(
        adapter_correction, "wide", split_axis=0, concat_axis=0, tiled=True
    )
    returned_rows = returned_rows.reshape(slot_count, column_portion)
    adapter_row_output = jnp.dot(
        placement.T, returned_rows, preferred_element_type=jnp.float32
    )
    return (base_projection_output + adapter_row_output).astype(jnp.bfloat16)


def solution(mesh):
    in_specs = (
        P("wide", "tensor"),
        P(None, "tensor"),
        P("tensor", "wide", None),
        P("wide", None, "tensor"),
        P("wide"),
        P(),
    )
    out_specs = P("wide", "tensor")
    return jax.shard_map(body, mesh=mesh, in_specs=in_specs, out_specs=out_specs, check_vma=False)
```

```python
import jax
import jax.numpy as jnp
from jax import lax
from jax.sharding import PartitionSpec as P


def body(
    tokens,
    key_value_weight,
    adapter_down_maps,
    adapter_up_maps,
    adapter_per_row,
    adapter_storage_slot,
):
    row_count, feature_portion = tokens.shape
    wide_count = lax.axis_size("wide")
    tensor_count = lax.axis_size("tensor")
    capacity = 2 * row_count // wide_count
    present_adapters = adapter_down_maps.shape[1]
    rank_dimension = adapter_down_maps.shape[2]
    column_portion = key_value_weight.shape[1]
    total_adapters = adapter_storage_slot.shape[0]
    slot_count = wide_count * capacity
    lane = 128
    info_rows = 8

    gathered = lax.all_gather(tokens, "tensor", axis=1, tiled=True)
    base_projection_output = jnp.dot(
        gathered, key_value_weight, preferred_element_type=jnp.float32
    )

    adapter_match = (
        adapter_per_row[:, None] == jnp.arange(total_adapters, dtype=jnp.int32)[None, :]
    ).astype(jnp.bfloat16)
    slot_parts = jnp.stack(
        [adapter_storage_slot // present_adapters, adapter_storage_slot % present_adapters], axis=1
    ).astype(jnp.bfloat16)
    picked = jnp.dot(adapter_match, slot_parts, preferred_element_type=jnp.float32)
    owner_index = picked[:, 0].astype(jnp.int32)
    local_index = picked[:, 1].astype(jnp.int32)

    owner_onehot = (
        owner_index[:, None] == jnp.arange(wide_count, dtype=jnp.int32)[None, :]
    ).astype(jnp.float32)
    row_iota = jnp.arange(row_count, dtype=jnp.int32)
    strictly_before = (row_iota[:, None] > row_iota[None, :]).astype(jnp.float32)
    earlier = jnp.dot(strictly_before, owner_onehot, preferred_element_type=jnp.float32)
    rank_in_owner = jnp.sum(earlier * owner_onehot, axis=1).astype(jnp.int32)
    destination = owner_index * capacity + rank_in_owner

    placement = lax.optimization_barrier(
        (jnp.arange(slot_count, dtype=jnp.int32)[:, None] == destination[None, :]).astype(
            jnp.bfloat16
        )
    )

    lane_tiles = feature_portion // lane
    local_code = jnp.broadcast_to(
        (local_index + 1).astype(jnp.bfloat16)[:, None], (row_count, lane)
    )
    placement_blocks = placement.reshape(wide_count, capacity, row_count)
    token_tiles = tokens.reshape(row_count, lane_tiles, lane)
    placed = jnp.einsum(
        "dcr,rjl->djcl", placement_blocks, token_tiles, preferred_element_type=jnp.float32
    ).astype(jnp.bfloat16)
    pieces = [placed.reshape(wide_count, lane_tiles * capacity, lane)]
    placed_code = jnp.dot(placement, local_code, preferred_element_type=jnp.float32)
    slot_code = placed_code[:, 0].astype(jnp.bfloat16).reshape(wide_count, 1, capacity)
    pieces.append(jnp.pad(slot_code, ((0, 0), (0, info_rows - 1), (0, lane - capacity))))
    send_block = jnp.concatenate(pieces, axis=1)

    got_block = lax.all_to_all(send_block, "wide", split_axis=0, concat_axis=0, tiled=True)
    flat_rows = jnp.concatenate(
        [
            got_block[:, tile * capacity : (tile + 1) * capacity, :].reshape(slot_count, lane)
            for tile in range(lane_tiles)
        ],
        axis=1,
    )
    got_code = (
        got_block[:, lane_tiles * capacity, :capacity].reshape(slot_count).astype(jnp.int32)
    )
    selected = (
        got_code[:, None] == jnp.arange(1, present_adapters + 1, dtype=jnp.int32)[None, :]
    )[:, :, None]

    down_matrix = adapter_down_maps.reshape(feature_portion, present_adapters * rank_dimension)
    all_ranks = jnp.dot(flat_rows, down_matrix, preferred_element_type=jnp.float32)
    all_ranks = all_ranks.reshape(slot_count, present_adapters, rank_dimension)
    partial_value = jnp.sum(jnp.where(selected, all_ranks, 0.0), axis=1)
    block_rows = slot_count // tensor_count
    dense_shape = (tensor_count, 8, block_rows * rank_dimension // 8)
    slot_blocks = partial_value.reshape(dense_shape)
    gathered_blocks = lax.all_to_all(slot_blocks, "tensor", split_axis=0, concat_axis=0, tiled=True)
    own_sum = jnp.sum(gathered_blocks, axis=0).astype(jnp.bfloat16)
    spread_shape = (tensor_count, 16, block_rows * rank_dimension // 16)
    spread = jnp.broadcast_to(own_sum.reshape(spread_shape[1:])[None], spread_shape)
    reduced_rows = lax.all_to_all(spread, "tensor", split_axis=0, concat_axis=0, tiled=True)
    reduced_rows = reduced_rows.reshape(slot_count, rank_dimension)

    base_tie = (base_projection_output[0, 0] * 0.0).astype(jnp.bfloat16)
    expanded_rows = jnp.where(
        selected, reduced_rows[:, None, :] + base_tie, jnp.zeros((), jnp.bfloat16)
    ).reshape(slot_count, present_adapters * rank_dimension)
    up_matrix = adapter_up_maps.reshape(present_adapters * rank_dimension, column_portion)
    adapter_correction = jnp.dot(
        expanded_rows, up_matrix, preferred_element_type=jnp.float32
    ).astype(jnp.bfloat16)
    adapter_correction = adapter_correction.reshape(wide_count, capacity, column_portion)
    returned_rows = lax.all_to_all(
        adapter_correction, "wide", split_axis=0, concat_axis=0, tiled=True
    )
    returned_rows = returned_rows.reshape(slot_count, column_portion)
    adapter_row_output = jnp.dot(
        placement.T, returned_rows, preferred_element_type=jnp.float32
    )
    return (base_projection_output + adapter_row_output).astype(jnp.bfloat16)


def solution(mesh):
    in_specs = (
        P("wide", "tensor"),
        P(None, "tensor"),
        P("tensor", "wide", None),
        P("wide", None, "tensor"),
        P("wide"),
        P(),
    )
    out_specs = P("wide", "tensor")
    return jax.shard_map(body, mesh=mesh, in_specs=in_specs, out_specs=out_specs, check_vma=False)
```

```python
import jax
import jax.numpy as jnp
from jax import lax
from jax.sharding import PartitionSpec as P


def body(
    tokens,
    key_value_weight,
    adapter_down_maps,
    adapter_up_maps,
    adapter_per_row,
    adapter_storage_slot,
):
    row_count, feature_portion = tokens.shape
    wide_count = lax.axis_size("wide")
    tensor_count = lax.axis_size("tensor")
    capacity = 2 * row_count // wide_count
    present_adapters = adapter_down_maps.shape[1]
    rank_dimension = adapter_down_maps.shape[2]
    column_portion = key_value_weight.shape[1]
    total_adapters = adapter_storage_slot.shape[0]
    slot_count = wide_count * capacity
    lane = 128
    info_rows = 8

    gathered = lax.all_gather(tokens, "tensor", axis=1, tiled=True)
    base_projection_output = jnp.dot(
        gathered, key_value_weight, preferred_element_type=jnp.float32
    )

    adapter_match = (
        adapter_per_row[:, None] == jnp.arange(total_adapters, dtype=jnp.int32)[None, :]
    ).astype(jnp.bfloat16)
    slot_parts = jnp.stack(
        [adapter_storage_slot // present_adapters, adapter_storage_slot % present_adapters], axis=1
    ).astype(jnp.bfloat16)
    picked = jnp.dot(adapter_match, slot_parts, preferred_element_type=jnp.float32)
    owner_index = picked[:, 0].astype(jnp.int32)
    local_index = picked[:, 1].astype(jnp.int32)

    owner_onehot = (
        owner_index[:, None] == jnp.arange(wide_count, dtype=jnp.int32)[None, :]
    ).astype(jnp.float32)
    row_iota = jnp.arange(row_count, dtype=jnp.int32)
    strictly_before = (row_iota[:, None] > row_iota[None, :]).astype(jnp.float32)
    earlier = jnp.dot(strictly_before, owner_onehot, preferred_element_type=jnp.float32)
    rank_in_owner = jnp.sum(earlier * owner_onehot, axis=1).astype(jnp.int32)
    destination = owner_index * capacity + rank_in_owner

    placement = (
        jnp.arange(slot_count, dtype=jnp.int32)[:, None] == destination[None, :]
    ).astype(jnp.bfloat16)

    lane_tiles = feature_portion // lane
    placement_blocks = placement.reshape(wide_count, capacity, row_count)
    token_tiles = tokens.reshape(row_count, lane_tiles, lane)
    placed = jnp.einsum(
        "dcr,rjl->djcl", placement_blocks, token_tiles, preferred_element_type=jnp.float32
    ).astype(jnp.bfloat16)
    pieces = [placed.reshape(wide_count, lane_tiles * capacity, lane)]
    slot_code = jnp.sum(
        jnp.where(placement > 0, (local_index + 1)[None, :], 0), axis=1
    ).astype(jnp.bfloat16).reshape(wide_count, 1, capacity)
    pieces.append(jnp.pad(slot_code, ((0, 0), (0, info_rows - 1), (0, lane - capacity))))
    send_block = jnp.concatenate(pieces, axis=1)

    got_block = lax.all_to_all(send_block, "wide", split_axis=0, concat_axis=0, tiled=True)
    flat_rows = jnp.concatenate(
        [
            got_block[:, tile * capacity : (tile + 1) * capacity, :].reshape(slot_count, lane)
            for tile in range(lane_tiles)
        ],
        axis=1,
    )
    got_code = (
        got_block[:, lane_tiles * capacity, :capacity].reshape(slot_count).astype(jnp.int32)
    )
    selected = (
        got_code[:, None] == jnp.arange(1, present_adapters + 1, dtype=jnp.int32)[None, :]
    )[:, :, None]

    down_matrix = adapter_down_maps.reshape(feature_portion, present_adapters * rank_dimension)
    all_ranks = jnp.dot(flat_rows, down_matrix, preferred_element_type=jnp.float32)
    all_ranks = all_ranks.reshape(slot_count, present_adapters, rank_dimension)
    partial_value = jnp.sum(jnp.where(selected, all_ranks, 0.0), axis=1)
    block_rows = slot_count // tensor_count
    dense_shape = (tensor_count, 8, block_rows * rank_dimension // 8)
    slot_blocks = partial_value.reshape(dense_shape)
    gathered_blocks = lax.all_to_all(slot_blocks, "tensor", split_axis=0, concat_axis=0, tiled=True)
    own_sum = jnp.sum(gathered_blocks, axis=0).astype(jnp.bfloat16)
    spread_shape = (tensor_count, 16, block_rows * rank_dimension // 16)
    spread = jnp.broadcast_to(own_sum.reshape(spread_shape[1:])[None], spread_shape)
    reduced_rows = lax.all_to_all(spread, "tensor", split_axis=0, concat_axis=0, tiled=True)
    reduced_rows = reduced_rows.reshape(slot_count, rank_dimension)

    base_tie = (base_projection_output[0, 0] * 0.0).astype(jnp.bfloat16)
    expanded_rows = jnp.where(
        selected, reduced_rows[:, None, :] + base_tie, jnp.zeros((), jnp.bfloat16)
    ).reshape(slot_count, present_adapters * rank_dimension)
    up_matrix = adapter_up_maps.reshape(present_adapters * rank_dimension, column_portion)
    adapter_correction = jnp.dot(
        expanded_rows, up_matrix, preferred_element_type=jnp.float32
    ).astype(jnp.bfloat16)
    adapter_correction = adapter_correction.reshape(wide_count, capacity, column_portion)
    returned_rows = lax.all_to_all(
        adapter_correction, "wide", split_axis=0, concat_axis=0, tiled=True
    )
    returned_rows = returned_rows.reshape(slot_count, column_portion)
    adapter_row_output = jnp.dot(
        placement.T, returned_rows, preferred_element_type=jnp.float32
    )
    return (base_projection_output + adapter_row_output).astype(jnp.bfloat16)


def solution(mesh):
    in_specs = (
        P("wide", "tensor"),
        P(None, "tensor"),
        P("tensor", "wide", None),
        P("wide", None, "tensor"),
        P("wide"),
        P(),
    )
    out_specs = P("wide", "tensor")
    return jax.shard_map(body, mesh=mesh, in_specs=in_specs, out_specs=out_specs, check_vma=False)
```
